128 devices in a mesh: section: 2 (over x_lo), tok: 8 (over x_hi, z), mdl: 8 (over y, core).
Axes of the slice: x: 4 (x_hi: 2, x_lo: 2; x = x_hi * 2 + x_lo), y: 4, z: 4, core: 2. Of those that a mesh axis runs over, the one named last changes fastest.
Arguments:
- layer_input: bfloat16 [2, 2048, 2048], P(None, 'tok'), may hold values from -6 to 6
- segment_ids: int32 [2, 2048], replicated, may hold values from 0 to 3, as said below
- route_ids: int32 [2, 2048, 6], P(None, ('tok', 'mdl')), may hold values from 0 to 63, all different within a row; in each aligned block of 32 rows (0 to 31, 32 to 63, ..., all dimensions but the last counted through in order) at most 4 rows name the same one
- route_weights: float32 [2, 2048, 6], P(None, ('tok', 'mdl')), may hold values from 0.1 to 0.5
- attn_gain: float32 [2048], replicated, may hold values from 0.5 to 1.5
- w_query: bfloat16 [2048, 3072], P(None, 'mdl'), may hold values from -6.629126 to 6.629126
- w_kv_down: bfloat16 [2048, 576], replicated, may hold values from -0.13258252 to 0.13258252
- latent_gain: float32 [512], replicated, may hold values from 0.5 to 1.5
- w_kv_up: bfloat16 [512, 4096], P(None, 'mdl'), may hold values from -0.25 to 0.25
- w_out: bfloat16 [2048, 2048], P('mdl'), may hold values from -0.125 to 0.125
- ffn_gain: float32 [2048], replicated, may hold values from 0.5 to 1.5
- w_shared_gate: bfloat16 [2048, 2048], P(None, 'mdl'), may hold values from -0.125 to 0.125
- w_shared_up: bfloat16 [2048, 2048], P(None, 'mdl'), may hold values from -0.125 to 0.125
- w_shared_down: bfloat16 [2048, 2048], P('mdl'), may hold values from -0.125 to 0.125
- w_expert_gate: bfloat16 [64, 2048, 768], P(('tok', 'mdl')), may hold values from -0.125 to 0.125
- w_expert_up: bfloat16 [64, 2048, 768], P(('tok', 'mdl')), may hold values from -0.125 to 0.125
- w_expert_down: bfloat16 [64, 768, 2048], P(('tok', 'mdl')), may hold values from -0.21875 to 0.21875
Outputs:
- layer_output: bfloat16 [2, 2048, 2048], P('section', ('tok', 'mdl'))
The draws below stay inside these ranges and needn't reach their ends.
Inputs may be any that keep to these rules, and one draw needn't show every extreme that they name: `segment_ids`: segment numbers never fall along a pack; each segment has 1 to 1024 tokens and one has exactly 1024. `route_ids`: each token names 6 different experts. In each aligned block of 32 tokens of a pack (the tokens of one device), no expert is named by more than 4 tokens, a bound that some block reaches.
All inputs are finite; a program needn't handle non-finite values.
Results may differ from the reference program's by a relative error of at most 0.02.
Values may be sent and summed in bfloat16 or wider, within the bound.
No kernel may reach another device: no remote copies, remote signals or barrier semaphores. Data moves between devices by JAX's collectives and lax.ppermute only.
A program may use at most 128 MiB of HBM per device.

```python
import math
import jax
import jax.numpy as jnp
import numpy as np
from jax import lax

D = 2048
HEADS = 16
NOPE = 128
ROPE = 64
VDIM = 128
LATENT = 512
FFE = 768
SHARED = 2048
TOPK = 6
MICRO = 2
SEGS = 4
PACK = 2048
LONGEST = 1024
R_DEV = 32
EXPERTS = 64
CAP = 4
BUF = 256


def common_direction(key):
    flips = jax.random.bernoulli(jax.random.fold_in(key, 91), 0.5, (D,))
    return jnp.where(flips, 1.0, -1.0).astype(jnp.float32)


def slow_pairs(key):
    half_width = ROPE // 2
    low_count = max(1, ROPE // 16)
    index_all = jnp.arange(ROPE, dtype=jnp.int32)
    pair_index = index_all % half_width
    flips = jax.random.bernoulli(jax.random.fold_in(key, 93), 0.5, (ROPE,))
    signs = jnp.where(flips, 1.0, -1.0).astype(jnp.float32)
    return jnp.where(pair_index >= half_width - low_count, signs, 0.0) / math.sqrt(2.0 * low_count)


def coupling_strength():
    return (100.0 * (NOPE + ROPE)) ** 0.25


def segment_layout(key):
    rest_tokens = PACK - LONGEST
    labels = jnp.arange(SEGS, dtype=jnp.int32)
    token_index = jnp.arange(PACK, dtype=jnp.int32)
    rows = []
    for batch_idx in range(MICRO):
        batch_key = jax.random.fold_in(key, 500 + batch_idx)
        shuffled = jax.random.permutation(jax.random.fold_in(batch_key, 1), rest_tokens - 1).astype(jnp.int32) + 1
        cuts = jnp.sort(shuffled[:SEGS - 2])
        bounds = jnp.concatenate([jnp.zeros((1,), jnp.int32), cuts, jnp.full((1,), rest_tokens, jnp.int32)])
        short_lengths = bounds[1:] - bounds[:-1]
        long_slot = jax.random.randint(jax.random.fold_in(batch_key, 2), (), 0, SEGS).astype(jnp.int32)
        before = jnp.clip(labels, 0, SEGS - 2)
        after = jnp.clip(labels - 1, 0, SEGS - 2)
        lengths = jnp.where(labels < long_slot, short_lengths[before], jnp.where(labels == long_slot, LONGEST, short_lengths[after])).astype(jnp.int32)
        starts = jnp.cumsum(lengths) - lengths
        ids = jnp.sum((token_index[:, None] >= starts[None, 1:]).astype(jnp.int32), axis=1)
        rows.append(ids)
    return jnp.stack(rows).astype(jnp.int32)


def draw_segment_ids(key, part):
    return segment_layout(key)


def draw_layer_input(key, part):
    segments = segment_layout(key)
    labels = jnp.arange(SEGS, dtype=jnp.int32)
    starts = jnp.sum((segments[:, None, :] < labels[None, :, None]).astype(jnp.int32), axis=2)
    first_rows = jnp.take_along_axis(starts, segments, axis=1)
    positions = jnp.arange(PACK, dtype=jnp.int32)[None, :] - first_rows
    opening = positions < 8
    noise = jnp.clip(jax.random.normal(jax.random.fold_in(key, 31), (MICRO, PACK, D), jnp.float32), -4.0, 4.0)
    strength = jnp.where(opening, 2.0, -0.5).astype(jnp.float32)
    rows = noise + strength[:, :, None] * common_direction(key)[None, None, :]
    return rows.astype(jnp.bfloat16)


def draw_w_query(key, part):
    base = jnp.clip(jax.random.normal(jax.random.fold_in(key, 13), (D, HEADS, NOPE + ROPE), jnp.float32), -5.0, 5.0) / math.sqrt(D)
    rope_cols = base[:, :, NOPE:]
    sink_term = coupling_strength() / D * common_direction(key)[:, None, None] * slow_pairs(key)[None, None, :]
    rope_cols = rope_cols - sink_term
    full = jnp.concatenate([base[:, :, :NOPE], rope_cols], axis=2)
    limit = 300.0 / math.sqrt(D)
    full = jnp.clip(full, -limit, limit)
    return full.reshape(D, HEADS * (NOPE + ROPE)).astype(jnp.bfloat16)


def draw_w_kv_down(key, part):
    base = jnp.clip(jax.random.normal(jax.random.fold_in(key, 11), (D, LATENT + ROPE), jnp.float32), -5.0, 5.0) / math.sqrt(D)
    rope_cols = base[:, LATENT:]
    sink_term = coupling_strength() / D * common_direction(key)[:, None] * slow_pairs(key)[None, :]
    rope_cols = rope_cols + sink_term
    return jnp.concatenate([base[:, :LATENT], rope_cols], axis=1).astype(jnp.bfloat16)


def steps_of(key, extent, split, low, high):
    level = 1.0
    for axis_at, blocks in split:
        steps = jax.random.uniform(jax.random.fold_in(jax.random.fold_in(key, 6), axis_at), (blocks,), jnp.float32, low / len(split), high / len(split))
        level = level * jnp.repeat(jnp.exp(steps), extent[axis_at] // blocks).reshape((-1,) + (1,) * (len(extent) - 1 - axis_at))
    return level


def deal_out(stream_key, own, number, rows, count, top, bound, slope):
    ranking = jax.random.permutation(stream_key, count)
    heavy_load, ordinary = load_shares(count, rows * top, bound, slope, True), load_shares(count, rows * top, bound, slope, False)
    places = jnp.arange(count)

    def named(sizes, rotation):
        used = int((sizes > 0).sum())
        fixed = max(1, used // 4)
        shifted = fixed + (places - fixed + rotation * (used - fixed)) % max(1, count - fixed)
        return jnp.zeros((count,), jnp.int32).at[ranking[jnp.where(places < fixed, places, shifted)]].set(jnp.asarray(sizes, jnp.int32))

    sizes = jnp.where(number % 4 == 0, named(heavy_load, number // 4), named(ordinary, number - number // 4 - 1))
    mixed = jax.random.permutation(jax.random.fold_in(own, 3), count)
    donor, taker = mixed[0:count // 2 * 2:2], mixed[1:count // 2 * 2:2]
    slack = jnp.minimum(sizes[donor] - 1, bound - sizes[taker]) // 2
    slack = jnp.where((donor == ranking[0]) | (taker == ranking[0]) | (sizes[taker] == 0), 0, jnp.maximum(slack, 0))
    shifted = jax.random.randint(jax.random.fold_in(own, 4), (count // 2,), 0, 1 << 20) % (slack + 1)
    sizes = sizes.at[donor].add(-shifted).at[taker].add(shifted)
    members = jnp.searchsorted(jnp.cumsum(sizes), jnp.arange(rows * top), side="right").astype(jnp.int32)
    listing = members.reshape(top, rows).T
    listing = listing[jax.random.permutation(jax.random.fold_in(own, 1), rows)]
    rotation = jax.random.randint(jax.random.fold_in(own, 2), (rows, 1), 0, top)
    return jnp.take_along_axis(listing, (jnp.arange(top)[None, :] + rotation) % top, axis=1)


def load_shares(amount, total, reach, skew, full):
    loads = [(1 << 20) // math.isqrt(standing ** skew) + 1 for standing in range(1, amount + 1)]
    largest = reach if full else min(reach, max(-(-total // amount), total * loads[0] // sum(loads)))
    least = 1 if total - largest >= amount - 1 else 0
    counts, rest = [largest] + [least] * (amount - 1), total - largest - least * (amount - 1)
    while rest > 0:
        candidates = [i for i in range(1, amount) if counts[i] < largest] or [i for i in range(1, amount) if counts[i] < reach]
        mass, remaining = sum([loads[i] for i in candidates]), rest
        for i in candidates:
            extra = min(reach - counts[i], max(1, remaining * loads[i] // mass), rest)
            counts[i] = counts[i] + extra
            rest = rest - extra
    return np.array(counts)


def centred(own_key, extent, deviation, most, split=(), kind=jnp.bfloat16):
    level = steps_of(own_key, extent, split, -0.22, 0.18) if split else 1.0
    array = jax.random.normal(own_key, extent, jnp.float32) * deviation * level
    return jnp.minimum(jnp.maximum(array, -most), most).astype(kind)


def setup_inputs(seed: int = 0) -> dict:
    streams_of = jax.random.split(jax.random.key(seed), 18)
    layer_input = draw_layer_input(jax.random.fold_in(streams_of[17], 71), 0)
    segment_ids = draw_segment_ids(jax.random.fold_in(streams_of[17], 71), 0)
    route_ids_keys = jax.random.split(jax.random.fold_in(streams_of[2], 1), MICRO * PACK // R_DEV)
    route_ids_turns = jax.random.permutation(jax.random.fold_in(streams_of[2], 3), MICRO * PACK // R_DEV)
    route_ids = jax.vmap(lambda own, number: deal_out(jax.random.fold_in(streams_of[2], 2), own, number, R_DEV, EXPERTS, TOPK, CAP, 2))(route_ids_keys, route_ids_turns).reshape((MICRO, PACK, TOPK))
    route_weights = jnp.clip(0.1 + 0.4 * jax.random.uniform(streams_of[3], (MICRO, PACK, TOPK), jnp.float32) ** steps_of(streams_of[3], (MICRO, PACK, TOPK), ((1, 64),), -0.2, 0.2), 0.1, 0.5)
    attn_gain = jnp.clip(1.0 + 0.1 * jax.random.normal(streams_of[4], (D,), jnp.float32), 0.5, 1.5)
    w_query = draw_w_query(jax.random.fold_in(streams_of[17], 71), 0)
    w_kv_down = draw_w_kv_down(jax.random.fold_in(streams_of[17], 71), 0)
    latent_gain = jnp.clip(1.0 + 0.1 * jax.random.normal(streams_of[7], (LATENT,), jnp.float32), 0.5, 1.5)
    w_kv_up = centred(streams_of[8], (LATENT, HEADS * (NOPE + VDIM)), LATENT ** -0.5, 0.25, ((1, 8),))
    w_out = centred(streams_of[9], (HEADS * VDIM, D), (HEADS * VDIM) ** -0.5, 0.125, ((0, 8),))
    ffn_gain = jnp.clip(1.0 + 0.1 * jax.random.normal(streams_of[10], (D,), jnp.float32), 0.5, 1.5)
    w_shared_gate = centred(streams_of[11], (D, SHARED), D ** -0.5, 0.125, ((1, 8),))
    w_shared_up = centred(streams_of[12], (D, SHARED), D ** -0.5, 0.125, ((1, 8),))
    w_shared_down = centred(streams_of[13], (SHARED, D), SHARED ** -0.5, 0.125, ((0, 8),))
    w_expert_gate = centred(streams_of[14], (EXPERTS, D, FFE), D ** -0.5, 0.125, ((0, 64),))
    w_expert_up = centred(streams_of[15], (EXPERTS, D, FFE), D ** -0.5, 0.125, ((0, 64),))
    w_expert_down = centred(streams_of[16], (EXPERTS, FFE, D), FFE ** -0.5, 0.21875, ((0, 64),))
    return {"layer_input": layer_input, "segment_ids": segment_ids, "route_ids": route_ids, "route_weights": route_weights, "attn_gain": attn_gain, "w_query": w_query, "w_kv_down": w_kv_down, "latent_gain": latent_gain, "w_kv_up": w_kv_up, "w_out": w_out, "ffn_gain": ffn_gain, "w_shared_gate": w_shared_gate, "w_shared_up": w_shared_up, "w_shared_down": w_shared_down, "w_expert_gate": w_expert_gate, "w_expert_up": w_expert_up, "w_expert_down": w_expert_down}


EPS = 1e-06

def rms_scale(values, gain_vec):
    values = values.astype(jnp.float32)
    return values * lax.rsqrt(lax.optimization_barrier(jnp.mean(values * values, axis=-1, keepdims=True)) + EPS) * gain_vec.astype(jnp.float32)

def rotary(values, positions):
    half_width = values.shape[-1] // 2
    frequency = 10000.0 ** (-jnp.arange(half_width, dtype=jnp.float32) / half_width)
    angles = positions.astype(jnp.float32)[:, None] * frequency[None, :]
    if values.ndim == 3:
        angles = angles[:, None, :]
    cosine = jnp.cos(angles)
    sine_part = jnp.sin(angles)
    lead_half = values[..., :half_width]
    tail_half = values[..., half_width:]
    return jnp.concatenate([lead_half * cosine - tail_half * sine_part, lead_half * sine_part + tail_half * cosine], axis=-1)

def attention_head(query_head, key_head, value_head, allowed, score_scale):
    scores = jnp.dot(query_head, key_head.T, preferred_element_type=jnp.float32) * score_scale
    masked = jnp.where(allowed, scores, -jnp.inf)
    running_max = lax.optimization_barrier(jnp.max(masked, axis=1, keepdims=True))
    weights = jnp.where(allowed, jnp.exp(scores - running_max), 0.0)
    totals = lax.optimization_barrier(jnp.sum(weights, axis=1, keepdims=True))
    summed = jnp.dot(weights.astype(jnp.bfloat16), value_head, preferred_element_type=jnp.float32)
    return (summed / totals).astype(jnp.bfloat16)

def one_batch(rows_in, segment_row, expert_ids, expert_weights, attn_gain, w_query, w_kv_down, latent_gain, w_kv_up, w_out, ffn_gain, w_shared_gate, w_shared_up, w_shared_down, w_expert_gate, w_expert_up, w_expert_down):
    labels = jnp.arange(SEGS, dtype=jnp.int32)
    starts = lax.optimization_barrier(jnp.sum((segment_row[None, :] < labels[:, None]).astype(jnp.int32), axis=1))
    token_index = jnp.arange(PACK, dtype=jnp.int32)
    positions = token_index - starts[segment_row]
    normed = rms_scale(rows_in, attn_gain).astype(jnp.bfloat16)
    queries = jnp.dot(normed, w_query, preferred_element_type=jnp.float32).reshape(PACK, HEADS, NOPE + ROPE)
    queries = jnp.concatenate([queries[..., :NOPE], rotary(queries[..., NOPE:], positions)], axis=-1).astype(jnp.bfloat16)
    compressed = jnp.dot(normed, w_kv_down, preferred_element_type=jnp.float32)
    latent = rms_scale(compressed[:, :LATENT], latent_gain).astype(jnp.bfloat16)
    key_rope = rotary(compressed[:, LATENT:], positions).astype(jnp.bfloat16)
    expanded = jnp.dot(latent, w_kv_up, preferred_element_type=jnp.float32).astype(jnp.bfloat16).reshape(PACK, HEADS, NOPE + VDIM)
    allowed = (segment_row[:, None] == segment_row[None, :]) & (token_index[None, :] <= token_index[:, None])
    score_scale = 1.0 / jnp.sqrt(jnp.float32(NOPE + ROPE))

    def per_head(head_inputs):
        query_head, nope_head, value_head = head_inputs
        key_head = jnp.concatenate([nope_head, key_rope], axis=-1)
        return attention_head(query_head, key_head, value_head, allowed, score_scale)
    heads_out = lax.map(per_head, (queries.transpose(1, 0, 2), expanded[..., :NOPE].transpose(1, 0, 2), expanded[..., NOPE:].transpose(1, 0, 2)))
    attended = heads_out.transpose(1, 0, 2).reshape(PACK, HEADS * VDIM)
    residual = (rows_in.astype(jnp.float32) + jnp.dot(attended, w_out, preferred_element_type=jnp.float32)).astype(jnp.bfloat16)
    normed_ffn = rms_scale(residual, ffn_gain).astype(jnp.bfloat16)
    shared_act = (jax.nn.silu(jnp.dot(normed_ffn, w_shared_gate, preferred_element_type=jnp.float32)) * jnp.dot(normed_ffn, w_shared_up, preferred_element_type=jnp.float32)).astype(jnp.bfloat16)
    shared_out = jnp.dot(shared_act, w_shared_down, preferred_element_type=jnp.float32)

    def expert_step(routed, expert):
        matched = expert_ids == expert
        row_weight = lax.optimization_barrier(jnp.sum(jnp.where(matched, expert_weights, 0.0), axis=1))
        chosen = jnp.any(matched, axis=1)
        chosen_count = jnp.sum(chosen.astype(jnp.int32))
        where_rows = jnp.nonzero(chosen, size=BUF, fill_value=0)[0].astype(jnp.int32)
        picked = normed_ffn[where_rows]
        gate_proj = jnp.dot(picked, w_expert_gate[expert], preferred_element_type=jnp.float32)
        up_proj = jnp.dot(picked, w_expert_up[expert], preferred_element_type=jnp.float32)
        expert_act = (jax.nn.silu(gate_proj) * up_proj).astype(jnp.bfloat16)
        expert_out = jnp.dot(expert_act, w_expert_down[expert], preferred_element_type=jnp.float32).astype(jnp.bfloat16)
        valid = jnp.arange(BUF, dtype=jnp.int32) < chosen_count
        scaling = jnp.where(valid, row_weight[where_rows], 0.0)
        routed = routed.at[where_rows].add(scaling[:, None] * expert_out.astype(jnp.float32))
        return (routed, None)
    routed, unused = lax.scan(expert_step, jnp.zeros((PACK, D), jnp.float32), jnp.arange(EXPERTS, dtype=jnp.int32))
    return (residual.astype(jnp.float32) + shared_out + routed).astype(jnp.bfloat16)

def reference(layer_input, segment_ids, route_ids, route_weights, attn_gain, w_query, w_kv_down, latent_gain, w_kv_up, w_out, ffn_gain, w_shared_gate, w_shared_up, w_shared_down, w_expert_gate, w_expert_up, w_expert_down):
    outputs = []
    for batch_idx in range(MICRO):
        outputs.append(one_batch(layer_input[batch_idx], segment_ids[batch_idx], route_ids[batch_idx], route_weights[batch_idx], attn_gain, w_query, w_kv_down, latent_gain, w_kv_up, w_out, ffn_gain, w_shared_gate, w_shared_up, w_shared_down, w_expert_gate, w_expert_up, w_expert_down))
    return jnp.stack(outputs)
```

```python
import math

import jax
import jax.numpy as jnp
from jax import lax
from jax.sharding import PartitionSpec as P

NOPE = 128
ROPE = 64
VDIM = 128
LATENT = 512
SEGS = 4


EPS = 1e-06


def passed_along(value, axis, steps):
    count = lax.axis_size(axis)
    initial, last = (max(0, -steps), min(count, count - steps))
    return lax.ppermute(value, axis, [(source, source + steps) for source in range(initial, last)])


def rms_scale(values, gain_vec):
    values = values.astype(jnp.float32)
    return values * lax.rsqrt(jnp.mean(values * values, axis=-1, keepdims=True) + EPS) * gain_vec


def rotary(values, positions):
    half_width = values.shape[-1] // 2
    frequency = 10000.0 ** (-jnp.arange(half_width, dtype=jnp.float32) / half_width)
    angles = positions.astype(jnp.float32)[:, None] * frequency[None, :]
    if values.ndim == 3:
        angles = angles[:, None, :]
    cosine = jnp.cos(angles)
    sine_part = jnp.sin(angles)
    lead_half = values[..., :half_width]
    tail_half = values[..., half_width:]
    return jnp.concatenate(
        [lead_half * cosine - tail_half * sine_part, lead_half * sine_part + tail_half * cosine],
        axis=-1,
    )


def positions_of(segment_row, segment_count):
    labels = jnp.arange(segment_count, dtype=jnp.int32)
    starts = jnp.sum((segment_row[None, :] < labels[:, None]).astype(jnp.int32), axis=1)
    member = (segment_row[:, None] == labels[None, :]).astype(jnp.int32)
    return jnp.arange(segment_row.shape[0], dtype=jnp.int32) - jnp.sum(
        member * starts[None, :], axis=1
    )


def shards(
    layer_input,
    segment_ids,
    route_ids,
    route_weights,
    attn_gain,
    w_query,
    w_kv_down,
    latent_gain,
    w_kv_up,
    w_out,
    ffn_gain,
    w_shared_gate,
    w_shared_up,
    w_shared_down,
    w_expert_gate,
    w_expert_up,
    w_expert_down,
):
    n_mdl = lax.axis_size("mdl")
    n_wide = lax.axis_size(("tok", "mdl"))
    section_id = lax.axis_index("section")
    tok_rank = lax.axis_index("tok")
    mdl_rank = lax.axis_index("mdl")
    micro_count, tok_dev, model_width = layer_input.shape
    row_dev = tok_dev // n_mdl
    top_count = route_ids.shape[2]
    local_heads = w_out.shape[0] // VDIM
    qk_width = NOPE + ROPE
    score_scale = 1.0 / math.sqrt(qk_width)
    expert_dev = w_expert_gate.shape[0]
    expert_total = expert_dev * n_wide
    capacity = max(2, 3 * row_dev * top_count // (2 * expert_total))
    slot_total = expert_total * capacity
    slot_ids = jnp.arange(slot_total, dtype=jnp.int32)
    expert_labels = jnp.arange(expert_total, dtype=jnp.int32)

    segment_row = lax.dynamic_index_in_dim(segment_ids, section_id, 0, keepdims=False)
    rows_in = lax.dynamic_index_in_dim(layer_input, section_id, 0, keepdims=False)
    expert_ids = lax.dynamic_index_in_dim(route_ids, section_id, 0, keepdims=False).reshape(-1)
    weight_rows = lax.dynamic_index_in_dim(route_weights, section_id, 0, keepdims=False)

    positions = positions_of(segment_row, SEGS)
    query_start = tok_rank * tok_dev
    query_pos = lax.dynamic_slice_in_dim(positions, query_start, tok_dev)
    query_seg = lax.dynamic_slice_in_dim(segment_row, query_start, tok_dev)
    query_index = query_start + jnp.arange(tok_dev, dtype=jnp.int32)

    normed = rms_scale(rows_in, attn_gain).astype(jnp.bfloat16)
    queries = jnp.dot(normed, w_query, preferred_element_type=jnp.float32).reshape(
        tok_dev, local_heads, qk_width
    )
    queries = jnp.concatenate(
        [queries[..., :NOPE], rotary(queries[..., NOPE:], query_pos)], axis=-1
    ).astype(jnp.bfloat16)
    compressed = jnp.dot(normed, w_kv_down, preferred_element_type=jnp.float32)
    latent = rms_scale(compressed[:, :LATENT], latent_gain).astype(jnp.bfloat16)
    key_rope = rotary(compressed[:, LATENT:], query_pos).astype(jnp.bfloat16)
    kv_rows = lax.all_gather(
        jnp.concatenate([latent, key_rope], axis=-1), "tok", axis=0, tiled=True
    )
    key_count = kv_rows.shape[0]
    expanded = (
        jnp.dot(kv_rows[:, :LATENT], w_kv_up, preferred_element_type=jnp.float32)
        .astype(jnp.bfloat16)
        .reshape(key_count, local_heads, NOPE + VDIM)
    )
    rope_keys = kv_rows[:, LATENT:]
    scores = jnp.einsum(
        "qhd,khd->hqk", queries[..., :NOPE], expanded[..., :NOPE],
        preferred_element_type=jnp.float32,
    )
    scores = scores + jnp.einsum(
        "qhd,kd->hqk", queries[..., NOPE:], rope_keys, preferred_element_type=jnp.float32
    )
    scores = scores * score_scale
    key_index = jnp.arange(key_count, dtype=jnp.int32)
    allowed = (segment_row[None, :] == query_seg[:, None]) & (
        key_index[None, :] <= query_index[:, None]
    )
    allowed = allowed[None, :, :]
    masked = jnp.where(allowed, scores, -1e30)
    row_max = jnp.max(masked, axis=-1, keepdims=True)
    weights = jnp.where(allowed, jnp.exp(scores - row_max), 0.0)
    totals = jnp.sum(weights, axis=-1, keepdims=True)
    weighted = jnp.einsum(
        "hqk,khd->hqd", weights.astype(jnp.bfloat16), expanded[..., NOPE:],
        preferred_element_type=jnp.float32,
    )
    attended = (
        (weighted / totals).astype(jnp.bfloat16).transpose(1, 0, 2).reshape(tok_dev, local_heads * VDIM)
    )
    mixed_heads = lax.psum(
        jnp.dot(attended, w_out, preferred_element_type=jnp.float32).astype(jnp.bfloat16), "mdl"
    ).astype(jnp.float32)
    residual = (rows_in.astype(jnp.float32) + mixed_heads).astype(jnp.bfloat16)
    normed_ffn_all = rms_scale(residual, ffn_gain).astype(jnp.bfloat16)
    own_residual = lax.dynamic_slice_in_dim(residual, mdl_rank * row_dev, row_dev)
    normed_ffn = lax.dynamic_slice_in_dim(normed_ffn_all, mdl_rank * row_dev, row_dev)

    gate_proj = jnp.dot(normed_ffn_all, w_shared_gate, preferred_element_type=jnp.float32)
    up_proj = jnp.dot(normed_ffn_all, w_shared_up, preferred_element_type=jnp.float32)
    shared_act = (jax.nn.silu(gate_proj) * up_proj).astype(jnp.bfloat16)
    shared_out = lax.psum_scatter(
        jnp.dot(shared_act, w_shared_down, preferred_element_type=jnp.float32).astype(jnp.bfloat16),
        "mdl",
        scatter_dimension=0,
        tiled=True,
    ).astype(jnp.float32)

    onehot = (expert_ids[:, None] == expert_labels[None, :]).astype(jnp.int32)
    earlier = jnp.cumsum(onehot, axis=0) - onehot
    slot_index = jnp.sum(earlier * onehot, axis=1)
    target = expert_ids * capacity + slot_index
    placing = (
        (slot_ids[:, None] == target[None, :])
        .astype(jnp.int32)
        .reshape(slot_total, row_dev, top_count)
    )
    placing = jnp.sum(placing, axis=2).astype(jnp.bfloat16)
    outgoing = (
        jnp.dot(placing, normed_ffn, preferred_element_type=jnp.float32)
        .astype(jnp.bfloat16)
        .reshape(expert_total, capacity, model_width)
    )
    buffer = lax.all_to_all(outgoing, ("tok", "mdl"), split_axis=0, concat_axis=0, tiled=True)
    item_count = buffer.shape[1]
    grouped = (
        buffer.reshape(n_wide, expert_dev, item_count, model_width)
        .transpose(1, 0, 2, 3)
        .reshape(expert_dev, n_wide * item_count, model_width)
    )
    e_gate = jnp.einsum("erd,edf->erf", grouped, w_expert_gate, preferred_element_type=jnp.float32)
    e_up = jnp.einsum("erd,edf->erf", grouped, w_expert_up, preferred_element_type=jnp.float32)
    expert_act = (jax.nn.silu(e_gate) * e_up).astype(jnp.bfloat16)
    produced = jnp.einsum(
        "erf,efd->erd", expert_act, w_expert_down, preferred_element_type=jnp.float32
    ).astype(jnp.bfloat16)
    processed = (
        produced.reshape(expert_dev, n_wide, item_count, model_width)
        .transpose(1, 0, 2, 3)
        .reshape(n_wide * expert_dev, item_count, model_width)
    )
    returned = lax.all_to_all(processed, ("tok", "mdl"), split_axis=0, concat_axis=0, tiled=True)
    matched = target.reshape(row_dev, top_count)[:, :, None] == slot_ids[None, None, :]
    combining = jnp.sum(jnp.where(matched, weight_rows[:, :, None], 0.0), axis=1)
    routed = jnp.dot(
        combining,
        returned.reshape(slot_total, model_width).astype(jnp.float32),
        precision=lax.Precision.HIGHEST,
    )
    finished = (own_residual.astype(jnp.float32) + shared_out + routed).astype(jnp.bfloat16)
    return finished[None]


def solution(mesh):
    in_specs = (
        P(None, "tok", None),
        P(),
        P(None, ("tok", "mdl"), None),
        P(None, ("tok", "mdl"), None),
        P(),
        P(None, "mdl"),
        P(),
        P(),
        P(None, "mdl"),
        P("mdl", None),
        P(),
        P(None, "mdl"),
        P(None, "mdl"),
        P("mdl", None),
        P(("tok", "mdl"), None, None),
        P(("tok", "mdl"), None, None),
        P(("tok", "mdl"), None, None),
    )
    out_specs = P("section", ("tok", "mdl"), None)
    return jax.shard_map(shards, mesh=mesh, in_specs=in_specs, out_specs=out_specs, check_vma=False)
```

```python
import math

import jax
import jax.numpy as jnp
from jax import lax
from jax.sharding import PartitionSpec as P

NOPE = 128
ROPE = 64
VDIM = 128
LATENT = 512
SEGS = 4
LONGEST_SEGMENT = 1024


EPS = 1e-06


def passed_along(value, axis, steps):
    count = lax.axis_size(axis)
    initial, last = (max(0, -steps), min(count, count - steps))
    return lax.ppermute(value, axis, [(source, source + steps) for source in range(initial, last)])


def summed_over(parts, axis):
    count = lax.axis_size(axis)
    pieces = parts.reshape((count, parts.shape[0] // count) + parts.shape[1:])
    arrived = lax.all_to_all(pieces, axis, 0, 0, tiled=True)
    return jnp.sum(arrived.astype(jnp.float32), axis=0)


def gathered_over(block, axis):
    count = lax.axis_size(axis)
    copies = jnp.broadcast_to(block[None], (count,) + block.shape)
    arrived = lax.all_to_all(copies, axis, 0, 0, tiled=True)
    return arrived.reshape((count * block.shape[0],) + block.shape[1:])


def rms_scale(values, gain_vec):
    values = values.astype(jnp.float32)
    return values * lax.rsqrt(jnp.mean(values * values, axis=-1, keepdims=True) + EPS) * gain_vec


def rotary(values, positions):
    half_width = values.shape[-1] // 2
    frequency = 10000.0 ** (-jnp.arange(half_width, dtype=jnp.float32) / half_width)
    angles = positions.astype(jnp.float32)[:, None] * frequency[None, :]
    if values.ndim == 3:
        angles = angles[:, None, :]
    cosine = jnp.cos(angles)
    sine_part = jnp.sin(angles)
    lead_half = values[..., :half_width]
    tail_half = values[..., half_width:]
    return jnp.concatenate(
        [lead_half * cosine - tail_half * sine_part, lead_half * sine_part + tail_half * cosine],
        axis=-1,
    )


def positions_of(segment_row, segment_count):
    labels = jnp.arange(segment_count, dtype=jnp.int32)
    starts = jnp.sum((segment_row[None, :] < labels[:, None]).astype(jnp.int32), axis=1)
    member = (segment_row[:, None] == labels[None, :]).astype(jnp.int32)
    return jnp.arange(segment_row.shape[0], dtype=jnp.int32) - jnp.sum(
        member * starts[None, :], axis=1
    )


def shards(
    layer_input,
    segment_ids,
    route_ids,
    route_weights,
    attn_gain,
    w_query,
    w_kv_down,
    latent_gain,
    w_kv_up,
    w_out,
    ffn_gain,
    w_shared_gate,
    w_shared_up,
    w_shared_down,
    w_expert_gate,
    w_expert_up,
    w_expert_down,
):
    n_mdl = lax.axis_size("mdl")
    n_wide = lax.axis_size(("tok", "mdl"))
    section_id = lax.axis_index("section")
    tok_rank = lax.axis_index("tok")
    mdl_rank = lax.axis_index("mdl")
    micro_count, tok_dev, model_width = layer_input.shape
    row_dev = tok_dev // n_mdl
    top_count = route_ids.shape[2]
    local_heads = w_out.shape[0] // VDIM
    qk_width = NOPE + ROPE
    score_scale = 1.0 / math.sqrt(qk_width)
    expert_dev = w_expert_gate.shape[0]
    expert_total = expert_dev * n_wide
    capacity = max(2, 3 * row_dev * top_count // (2 * expert_total))
    slot_total = expert_total * capacity
    slot_ids = jnp.arange(slot_total, dtype=jnp.int32)
    expert_labels = jnp.arange(expert_total, dtype=jnp.int32)

    segment_row = lax.dynamic_index_in_dim(segment_ids, section_id, 0, keepdims=False)
    rows_in = lax.dynamic_index_in_dim(layer_input, section_id, 0, keepdims=False)
    expert_ids = lax.dynamic_index_in_dim(route_ids, section_id, 0, keepdims=False).reshape(-1)
    weight_rows = lax.dynamic_index_in_dim(route_weights, section_id, 0, keepdims=False)

    positions = positions_of(segment_row, SEGS)
    query_start = tok_rank * tok_dev
    query_pos = lax.dynamic_slice_in_dim(positions, query_start, tok_dev)
    query_seg = lax.dynamic_slice_in_dim(segment_row, query_start, tok_dev)
    query_index = query_start + jnp.arange(tok_dev, dtype=jnp.int32)

    normed = rms_scale(rows_in, attn_gain).astype(jnp.bfloat16)
    queries = jnp.dot(normed, w_query, preferred_element_type=jnp.float32).reshape(
        tok_dev, local_heads, qk_width
    )
    queries = jnp.concatenate(
        [queries[..., :NOPE], rotary(queries[..., NOPE:], query_pos)], axis=-1
    ).astype(jnp.bfloat16)
    compressed = jnp.dot(normed, w_kv_down, preferred_element_type=jnp.float32)
    latent = rms_scale(compressed[:, :LATENT], latent_gain).astype(jnp.bfloat16)
    key_rope = rotary(compressed[:, LATENT:], query_pos).astype(jnp.bfloat16)
    n_tok = lax.axis_size("tok")
    reach = LONGEST_SEGMENT // tok_dev
    kv_own = jnp.concatenate([latent, key_rope], axis=-1)
    kv_parts = [kv_own]
    for steps in range(1, min(reach, n_tok - 1) + 1):
        kv_parts.insert(0, passed_along(kv_own, "tok", steps))
    kv_rows = jnp.concatenate(kv_parts, axis=0)
    key_count = kv_rows.shape[0]
    key_start = query_start + tok_dev - key_count
    expanded = (
        jnp.dot(kv_rows[:, :LATENT], w_kv_up, preferred_element_type=jnp.float32)
        .astype(jnp.bfloat16)
        .reshape(key_count, local_heads, NOPE + VDIM)
    )
    rope_keys = kv_rows[:, LATENT:]
    scores = jnp.einsum(
        "qhd,khd->hqk", queries[..., :NOPE], expanded[..., :NOPE],
        preferred_element_type=jnp.float32,
    )
    scores = scores + jnp.einsum(
        "qhd,kd->hqk", queries[..., NOPE:], rope_keys, preferred_element_type=jnp.float32
    )
    scores = scores * score_scale
    key_index = key_start + jnp.arange(key_count, dtype=jnp.int32)
    padded_seg = jnp.concatenate([jnp.full((key_count,), -1, jnp.int32), segment_row])
    key_seg = lax.dynamic_slice_in_dim(padded_seg, key_start + key_count, key_count)
    allowed = (
        (key_seg[None, :] == query_seg[:, None])
        & (key_index[None, :] <= query_index[:, None])
        & (key_index[None, :] >= 0)
    )
    allowed = allowed[None, :, :]
    masked = jnp.where(allowed, scores, -1e30)
    row_max = jnp.max(masked, axis=-1, keepdims=True)
    weights = jnp.where(allowed, jnp.exp(scores - row_max), 0.0)
    totals = jnp.sum(weights, axis=-1, keepdims=True)
    weighted = jnp.einsum(
        "hqk,khd->hqd", weights.astype(jnp.bfloat16), expanded[..., NOPE:],
        preferred_element_type=jnp.float32,
    )
    attended = (
        (weighted / totals).astype(jnp.bfloat16).transpose(1, 0, 2).reshape(tok_dev, local_heads * VDIM)
    )
    head_parts = jnp.dot(attended, w_out, preferred_element_type=jnp.float32).astype(jnp.bfloat16)
    mixed_heads = summed_over(head_parts, "mdl")
    own_input = lax.dynamic_slice_in_dim(rows_in, mdl_rank * row_dev, row_dev)
    own_residual = (own_input.astype(jnp.float32) + mixed_heads).astype(jnp.bfloat16)
    normed_ffn = rms_scale(own_residual, ffn_gain).astype(jnp.bfloat16)
    normed_ffn_all = gathered_over(normed_ffn, "mdl")

    gate_proj = jnp.dot(normed_ffn_all, w_shared_gate, preferred_element_type=jnp.float32)
    up_proj = jnp.dot(normed_ffn_all, w_shared_up, preferred_element_type=jnp.float32)
    shared_act = (jax.nn.silu(gate_proj) * up_proj).astype(jnp.bfloat16)
    shared_out = summed_over(
        jnp.dot(shared_act, w_shared_down, preferred_element_type=jnp.float32).astype(jnp.bfloat16),
        "mdl",
    )

    onehot = (expert_ids[:, None] == expert_labels[None, :]).astype(jnp.int32)
    earlier = jnp.cumsum(onehot, axis=0) - onehot
    slot_index = jnp.sum(earlier * onehot, axis=1)
    target = expert_ids * capacity + slot_index
    placing = (
        (slot_ids[:, None] == target[None, :])
        .astype(jnp.int32)
        .reshape(slot_total, row_dev, top_count)
    )
    placing = jnp.sum(placing, axis=2).astype(jnp.bfloat16)
    outgoing = (
        jnp.dot(placing, normed_ffn, preferred_element_type=jnp.float32)
        .astype(jnp.bfloat16)
        .reshape(expert_total, capacity, model_width)
    )
    buffer = lax.all_to_all(outgoing, ("tok", "mdl"), split_axis=0, concat_axis=0, tiled=True)
    item_count = buffer.shape[1]
    grouped = (
        buffer.reshape(n_wide, expert_dev, item_count, model_width)
        .transpose(1, 0, 2, 3)
        .reshape(expert_dev, n_wide * item_count, model_width)
    )
    e_gate = jnp.einsum("erd,edf->erf", grouped, w_expert_gate, preferred_element_type=jnp.float32)
    e_up = jnp.einsum("erd,edf->erf", grouped, w_expert_up, preferred_element_type=jnp.float32)
    expert_act = (jax.nn.silu(e_gate) * e_up).astype(jnp.bfloat16)
    produced = jnp.einsum(
        "erf,efd->erd", expert_act, w_expert_down, preferred_element_type=jnp.float32
    ).astype(jnp.bfloat16)
    processed = (
        produced.reshape(expert_dev, n_wide, item_count, model_width)
        .transpose(1, 0, 2, 3)
        .reshape(n_wide * expert_dev, item_count, model_width)
    )
    returned = lax.all_to_all(processed, ("tok", "mdl"), split_axis=0, concat_axis=0, tiled=True)
    matched = target.reshape(row_dev, top_count)[:, :, None] == slot_ids[None, None, :]
    combining = jnp.sum(jnp.where(matched, weight_rows[:, :, None], 0.0), axis=1)
    routed = jnp.dot(
        combining,
        returned.reshape(slot_total, model_width).astype(jnp.float32),
        precision=lax.Precision.HIGHEST,
    )
    finished = (own_residual.astype(jnp.float32) + shared_out + routed).astype(jnp.bfloat16)
    return finished[None]


def solution(mesh):
    in_specs = (
        P(None, "tok", None),
        P(),
        P(None, ("tok", "mdl"), None),
        P(None, ("tok", "mdl"), None),
        P(),
        P(None, "mdl"),
        P(),
        P(),
        P(None, "mdl"),
        P("mdl", None),
        P(),
        P(None, "mdl"),
        P(None, "mdl"),
        P("mdl", None),
        P(("tok", "mdl"), None, None),
        P(("tok", "mdl"), None, None),
        P(("tok", "mdl"), None, None),
    )
    out_specs = P("section", ("tok", "mdl"), None)
    return jax.shard_map(shards, mesh=mesh, in_specs=in_specs, out_specs=out_specs, check_vma=False)
```

```python
import math

import jax
import jax.numpy as jnp
from jax import lax
from jax.sharding import PartitionSpec as P

NOPE = 128
ROPE = 64
VDIM = 128
LATENT = 512
SEGS = 4
LONGEST_SEGMENT = 1024


EPS = 1e-06


def passed_along(value, axis, steps):
    count = lax.axis_size(axis)
    initial, last = (max(0, -steps), min(count, count - steps))
    return lax.ppermute(value, axis, [(source, source + steps) for source in range(initial, last)])


def summed_over(parts, axis, arrival_order=False):
    count = lax.axis_size(axis)
    rank = lax.axis_index(axis)
    pieces = parts.reshape((count, parts.shape[0] // count) + parts.shape[1:])

    def piece_for(steps):
        if arrival_order:
            return pieces[(count - steps) % count]
        return lax.dynamic_index_in_dim(pieces, (rank + steps) % count, 0, keepdims=False)

    total = piece_for(0).astype(jnp.float32)
    for steps in range(1, count):
        moved = lax.ppermute(piece_for(steps), axis, [(i, (i + steps) % count) for i in range(count)])
        total = total + moved.astype(jnp.float32)
    return total


def gathered_over(block, axis):
    count = lax.axis_size(axis)
    arrived = [block]
    for steps in range(1, count):
        arrived.append(lax.ppermute(block, axis, [(i, (i + steps) % count) for i in range(count)]))
    return jnp.concatenate(arrived, axis=0)


def rms_scale(values, gain_vec):
    values = values.astype(jnp.float32)
    return values * lax.rsqrt(jnp.mean(values * values, axis=-1, keepdims=True) + EPS) * gain_vec


def rotary(values, positions):
    half_width = values.shape[-1] // 2
    frequency = 10000.0 ** (-jnp.arange(half_width, dtype=jnp.float32) / half_width)
    angles = positions.astype(jnp.float32)[:, None] * frequency[None, :]
    if values.ndim == 3:
        angles = angles[:, None, :]
    cosine = jnp.cos(angles)
    sine_part = jnp.sin(angles)
    lead_half = values[..., :half_width]
    tail_half = values[..., half_width:]
    return jnp.concatenate(
        [lead_half * cosine - tail_half * sine_part, lead_half * sine_part + tail_half * cosine],
        axis=-1,
    )


def positions_of(segment_row, segment_count):
    labels = jnp.arange(segment_count, dtype=jnp.int32)
    starts = jnp.sum((segment_row[None, :] < labels[:, None]).astype(jnp.int32), axis=1)
    member = (segment_row[:, None] == labels[None, :]).astype(jnp.int32)
    return jnp.arange(segment_row.shape[0], dtype=jnp.int32) - jnp.sum(
        member * starts[None, :], axis=1
    )


def shards(
    layer_input,
    segment_ids,
    route_ids,
    route_weights,
    attn_gain,
    w_query,
    w_kv_down,
    latent_gain,
    w_kv_up,
    w_out,
    ffn_gain,
    w_shared_gate,
    w_shared_up,
    w_shared_down,
    w_expert_gate,
    w_expert_up,
    w_expert_down,
):
    n_mdl = lax.axis_size("mdl")
    n_wide = lax.axis_size(("tok", "mdl"))
    section_id = lax.axis_index("section")
    tok_rank = lax.axis_index("tok")
    mdl_rank = lax.axis_index("mdl")
    micro_count, tok_dev, model_width = layer_input.shape
    row_dev = tok_dev // n_mdl
    top_count = route_ids.shape[2]
    local_heads = w_out.shape[0] // VDIM
    qk_width = NOPE + ROPE
    score_scale = 1.0 / math.sqrt(qk_width)
    expert_dev = w_expert_gate.shape[0]
    expert_total = expert_dev * n_wide
    capacity = max(2, 3 * row_dev * top_count // (2 * expert_total))
    slot_total = expert_total * capacity
    slot_ids = jnp.arange(slot_total, dtype=jnp.int32)
    expert_labels = jnp.arange(expert_total, dtype=jnp.int32)

    segment_row = lax.dynamic_index_in_dim(segment_ids, section_id, 0, keepdims=False)
    rows_in = lax.dynamic_index_in_dim(layer_input, section_id, 0, keepdims=False)
    expert_ids = lax.dynamic_index_in_dim(route_ids, section_id, 0, keepdims=False).reshape(-1)
    weight_rows = lax.dynamic_index_in_dim(route_weights, section_id, 0, keepdims=False)

    positions = positions_of(segment_row, SEGS)
    query_start = tok_rank * tok_dev
    query_pos = lax.dynamic_slice_in_dim(positions, query_start, tok_dev)
    query_seg = lax.dynamic_slice_in_dim(segment_row, query_start, tok_dev)
    query_index = query_start + jnp.arange(tok_dev, dtype=jnp.int32)

    normed = rms_scale(rows_in, attn_gain).astype(jnp.bfloat16)
    queries = jnp.dot(normed, w_query, preferred_element_type=jnp.float32).reshape(
        tok_dev, local_heads, qk_width
    )
    queries = jnp.concatenate(
        [queries[..., :NOPE], rotary(queries[..., NOPE:], query_pos)], axis=-1
    ).astype(jnp.bfloat16)
    compressed = jnp.dot(normed, w_kv_down, preferred_element_type=jnp.float32)
    latent = rms_scale(compressed[:, :LATENT], latent_gain).astype(jnp.bfloat16)
    key_rope = rotary(compressed[:, LATENT:], query_pos).astype(jnp.bfloat16)
    n_tok = lax.axis_size("tok")
    reach = LONGEST_SEGMENT // tok_dev
    kv_own = jnp.concatenate([latent, key_rope], axis=-1)
    kv_parts = [kv_own]
    for steps in range(1, min(reach, n_tok - 1) + 1):
        kv_parts.insert(0, passed_along(kv_own, "tok", steps))
    kv_rows = jnp.concatenate(kv_parts, axis=0)
    key_count = kv_rows.shape[0]
    key_start = query_start + tok_dev - key_count
    expanded = (
        jnp.dot(kv_rows[:, :LATENT], w_kv_up, preferred_element_type=jnp.float32)
        .astype(jnp.bfloat16)
        .reshape(key_count, local_heads, NOPE + VDIM)
    )
    rope_keys = kv_rows[:, LATENT:]
    scores = jnp.einsum(
        "qhd,khd->hqk", queries[..., :NOPE], expanded[..., :NOPE],
        preferred_element_type=jnp.float32,
    )
    scores = scores + jnp.einsum(
        "qhd,kd->hqk", queries[..., NOPE:], rope_keys, preferred_element_type=jnp.float32
    )
    scores = scores * score_scale
    key_index = key_start + jnp.arange(key_count, dtype=jnp.int32)
    padded_seg = jnp.concatenate([jnp.full((key_count,), -1, jnp.int32), segment_row])
    key_seg = lax.dynamic_slice_in_dim(padded_seg, key_start + key_count, key_count)
    allowed = (
        (key_seg[None, :] == query_seg[:, None])
        & (key_index[None, :] <= query_index[:, None])
        & (key_index[None, :] >= 0)
    )
    allowed = allowed[None, :, :]
    masked = jnp.where(allowed, scores, -1e30)
    row_max = jnp.max(masked, axis=-1, keepdims=True)
    weights = jnp.where(allowed, jnp.exp(scores - row_max), 0.0)
    totals = jnp.sum(weights, axis=-1, keepdims=True)
    weighted = jnp.einsum(
        "hqk,khd->hqd", weights.astype(jnp.bfloat16), expanded[..., NOPE:],
        preferred_element_type=jnp.float32,
    )
    attended = (
        (weighted / totals).astype(jnp.bfloat16).transpose(1, 0, 2).reshape(tok_dev, local_heads * VDIM)
    )
    head_parts = jnp.dot(attended, w_out, preferred_element_type=jnp.float32).astype(jnp.bfloat16)
    mixed_heads = summed_over(head_parts, "mdl")
    own_input = lax.dynamic_slice_in_dim(rows_in, mdl_rank * row_dev, row_dev)
    own_residual = (own_input.astype(jnp.float32) + mixed_heads).astype(jnp.bfloat16)
    normed_ffn = rms_scale(own_residual, ffn_gain).astype(jnp.bfloat16)
    normed_ffn_all = gathered_over(normed_ffn, "mdl")

    gate_proj = jnp.dot(normed_ffn_all, w_shared_gate, preferred_element_type=jnp.float32)
    up_proj = jnp.dot(normed_ffn_all, w_shared_up, preferred_element_type=jnp.float32)
    shared_act = (jax.nn.silu(gate_proj) * up_proj).astype(jnp.bfloat16)
    shared_out = summed_over(
        jnp.dot(shared_act, w_shared_down, preferred_element_type=jnp.float32).astype(jnp.bfloat16),
        "mdl",
        arrival_order=True,
    )

    onehot = (expert_ids[:, None] == expert_labels[None, :]).astype(jnp.int32)
    earlier = jnp.cumsum(onehot, axis=0) - onehot
    slot_index = jnp.sum(earlier * onehot, axis=1)
    target = expert_ids * capacity + slot_index
    placing = (
        (slot_ids[:, None] == target[None, :])
        .astype(jnp.int32)
        .reshape(slot_total, row_dev, top_count)
    )
    placing = jnp.sum(placing, axis=2).astype(jnp.bfloat16)
    outgoing = (
        jnp.dot(placing, normed_ffn, preferred_element_type=jnp.float32)
        .astype(jnp.bfloat16)
        .reshape(expert_total, capacity, model_width)
    )
    buffer = lax.all_to_all(outgoing, ("tok", "mdl"), split_axis=0, concat_axis=0, tiled=True)
    item_count = buffer.shape[1]
    grouped = (
        buffer.reshape(n_wide, expert_dev, item_count, model_width)
        .transpose(1, 0, 2, 3)
        .reshape(expert_dev, n_wide * item_count, model_width)
    )
    e_gate = jnp.einsum("erd,edf->erf", grouped, w_expert_gate, preferred_element_type=jnp.float32)
    e_up = jnp.einsum("erd,edf->erf", grouped, w_expert_up, preferred_element_type=jnp.float32)
    expert_act = (jax.nn.silu(e_gate) * e_up).astype(jnp.bfloat16)
    produced = jnp.einsum(
        "erf,efd->erd", expert_act, w_expert_down, preferred_element_type=jnp.float32
    ).astype(jnp.bfloat16)
    processed = (
        produced.reshape(expert_dev, n_wide, item_count, model_width)
        .transpose(1, 0, 2, 3)
        .reshape(n_wide * expert_dev, item_count, model_width)
    )
    returned = lax.all_to_all(processed, ("tok", "mdl"), split_axis=0, concat_axis=0, tiled=True)
    matched = target.reshape(row_dev, top_count)[:, :, None] == slot_ids[None, None, :]
    combining = jnp.sum(jnp.where(matched, weight_rows[:, :, None], 0.0), axis=1)
    routed = jnp.dot(
        combining,
        returned.reshape(slot_total, model_width).astype(jnp.float32),
        precision=lax.Precision.HIGHEST,
    )
    finished = (own_residual.astype(jnp.float32) + shared_out + routed).astype(jnp.bfloat16)
    return finished[None]


def solution(mesh):
    in_specs = (
        P(None, "tok", None),
        P(),
        P(None, ("tok", "mdl"), None),
        P(None, ("tok", "mdl"), None),
        P(),
        P(None, "mdl"),
        P(),
        P(),
        P(None, "mdl"),
        P("mdl", None),
        P(),
        P(None, "mdl"),
        P(None, "mdl"),
        P("mdl", None),
        P(("tok", "mdl"), None, None),
        P(("tok", "mdl"), None, None),
        P(("tok", "mdl"), None, None),
    )
    out_specs = P("section", ("tok", "mdl"), None)
    return jax.shard_map(shards, mesh=mesh, in_specs=in_specs, out_specs=out_specs, check_vma=False)
```

```python
import math

import jax
import jax.numpy as jnp
from jax import lax
from jax.sharding import PartitionSpec as P

NOPE = 128
ROPE = 64
VDIM = 128
LATENT = 512
SEGS = 4
LONGEST_SEGMENT = 1024


EPS = 1e-06


def passed_along(value, axis, steps):
    count = lax.axis_size(axis)
    initial, last = (max(0, -steps), min(count, count - steps))
    return lax.ppermute(value, axis, [(source, source + steps) for source in range(initial, last)])


def summed_over(parts, axis, arrival_order=False):
    count = lax.axis_size(axis)
    rank = lax.axis_index(axis)
    pieces = parts.reshape((count, parts.shape[0] // count) + parts.shape[1:])

    def piece_for(steps):
        if arrival_order:
            return pieces[(count - steps) % count]
        return lax.dynamic_index_in_dim(pieces, (rank + steps) % count, 0, keepdims=False)

    total = piece_for(0).astype(jnp.float32)
    for steps in range(1, count):
        moved = lax.ppermute(piece_for(steps), axis, [(i, (i + steps) % count) for i in range(count)])
        total = total + moved.astype(jnp.float32)
    return total


def gathered_over(block, axis):
    count = lax.axis_size(axis)
    arrived = [block]
    for steps in range(1, count):
        arrived.append(lax.ppermute(block, axis, [(i, (i + steps) % count) for i in range(count)]))
    return jnp.concatenate(arrived, axis=0)


def rms_scale(values, gain_vec):
    values = values.astype(jnp.float32)
    return values * lax.rsqrt(jnp.mean(values * values, axis=-1, keepdims=True) + EPS) * gain_vec


def rotary(values, positions):
    half_width = values.shape[-1] // 2
    frequency = 10000.0 ** (-jnp.arange(half_width, dtype=jnp.float32) / half_width)
    angles = positions.astype(jnp.float32)[:, None] * frequency[None, :]
    if values.ndim == 3:
        angles = angles[:, None, :]
    cosine = jnp.cos(angles)
    sine_part = jnp.sin(angles)
    lead_half = values[..., :half_width]
    tail_half = values[..., half_width:]
    return jnp.concatenate(
        [lead_half * cosine - tail_half * sine_part, lead_half * sine_part + tail_half * cosine],
        axis=-1,
    )


def positions_of(segment_row, segment_count):
    labels = jnp.arange(segment_count, dtype=jnp.int32)
    starts = jnp.sum((segment_row[None, :] < labels[:, None]).astype(jnp.int32), axis=1)
    member = (segment_row[:, None] == labels[None, :]).astype(jnp.int32)
    return jnp.arange(segment_row.shape[0], dtype=jnp.int32) - jnp.sum(
        member * starts[None, :], axis=1
    )


def shards(
    layer_input,
    segment_ids,
    route_ids,
    route_weights,
    attn_gain,
    w_query,
    w_kv_down,
    latent_gain,
    w_kv_up,
    w_out,
    ffn_gain,
    w_shared_gate,
    w_shared_up,
    w_shared_down,
    w_expert_gate,
    w_expert_up,
    w_expert_down,
):
    n_mdl = lax.axis_size("mdl")
    n_wide = lax.axis_size(("tok", "mdl"))
    section_id = lax.axis_index("section")
    tok_rank = lax.axis_index("tok")
    mdl_rank = lax.axis_index("mdl")
    micro_count, tok_dev, model_width = layer_input.shape
    row_dev = tok_dev // n_mdl
    top_count = route_ids.shape[2]
    local_heads = w_out.shape[0] // VDIM
    qk_width = NOPE + ROPE
    score_scale = 1.0 / math.sqrt(qk_width)
    expert_dev = w_expert_gate.shape[0]
    expert_total = expert_dev * n_wide
    capacity = max(2, 3 * row_dev * top_count // (2 * expert_total))
    slot_total = expert_total * capacity
    slot_ids = jnp.arange(slot_total, dtype=jnp.int32)
    expert_labels = jnp.arange(expert_total, dtype=jnp.int32)

    segment_row = lax.dynamic_index_in_dim(segment_ids, section_id, 0, keepdims=False)
    rows_in = lax.dynamic_index_in_dim(layer_input, section_id, 0, keepdims=False)
    expert_ids = lax.dynamic_index_in_dim(route_ids, section_id, 0, keepdims=False).reshape(-1)
    weight_rows = lax.dynamic_index_in_dim(route_weights, section_id, 0, keepdims=False)

    positions = positions_of(segment_row, SEGS)
    query_start = tok_rank * tok_dev
    query_pos = lax.dynamic_slice_in_dim(positions, query_start, tok_dev)
    query_seg = lax.dynamic_slice_in_dim(segment_row, query_start, tok_dev)
    query_index = query_start + jnp.arange(tok_dev, dtype=jnp.int32)

    normed = rms_scale(rows_in, attn_gain).astype(jnp.bfloat16)
    queries = jnp.dot(normed, w_query, preferred_element_type=jnp.float32).reshape(
        tok_dev, local_heads, qk_width
    )
    queries = jnp.concatenate(
        [queries[..., :NOPE], rotary(queries[..., NOPE:], query_pos)], axis=-1
    ).astype(jnp.bfloat16)
    compressed = jnp.dot(normed, w_kv_down, preferred_element_type=jnp.float32)
    latent = rms_scale(compressed[:, :LATENT], latent_gain).astype(jnp.bfloat16)
    key_rope = rotary(compressed[:, LATENT:], query_pos).astype(jnp.bfloat16)
    n_tok = lax.axis_size("tok")
    reach = LONGEST_SEGMENT // tok_dev
    kv_own = jnp.concatenate([latent, key_rope], axis=-1)
    kv_parts = [kv_own]
    for steps in range(1, min(reach, n_tok - 1) + 1):
        kv_parts.insert(0, passed_along(kv_own, "tok", steps))
    kv_rows = jnp.concatenate(kv_parts, axis=0)
    key_count = kv_rows.shape[0]
    key_start = query_start + tok_dev - key_count
    expanded = (
        jnp.dot(kv_rows[:, :LATENT], w_kv_up, preferred_element_type=jnp.float32)
        .astype(jnp.bfloat16)
        .reshape(key_count, local_heads, NOPE + VDIM)
    )
    rope_keys = kv_rows[:, LATENT:]
    scores = jnp.einsum(
        "qhd,khd->hqk", queries[..., :NOPE], expanded[..., :NOPE],
        preferred_element_type=jnp.float32,
    )
    scores = scores + jnp.einsum(
        "qhd,kd->hqk", queries[..., NOPE:], rope_keys, preferred_element_type=jnp.float32
    )
    scores = scores * score_scale
    key_index = key_start + jnp.arange(key_count, dtype=jnp.int32)
    padded_seg = jnp.concatenate([jnp.full((key_count,), -1, jnp.int32), segment_row])
    key_seg = lax.dynamic_slice_in_dim(padded_seg, key_start + key_count, key_count)
    allowed = (
        (key_seg[None, :] == query_seg[:, None])
        & (key_index[None, :] <= query_index[:, None])
        & (key_index[None, :] >= 0)
    )
    allowed = allowed[None, :, :]
    masked = jnp.where(allowed, scores, -1e30)
    row_max = jnp.max(masked, axis=-1, keepdims=True)
    weights = jnp.where(allowed, jnp.exp(scores - row_max), 0.0)
    totals = jnp.sum(weights, axis=-1, keepdims=True)
    weighted = jnp.einsum(
        "hqk,khd->hqd", weights.astype(jnp.bfloat16), expanded[..., NOPE:],
        preferred_element_type=jnp.float32,
    )
    attended = (
        (weighted / totals).astype(jnp.bfloat16).transpose(1, 0, 2).reshape(tok_dev, local_heads * VDIM)
    )
    head_parts = jnp.dot(attended, w_out, preferred_element_type=jnp.float32).astype(jnp.bfloat16)
    mixed_heads = summed_over(head_parts, "mdl")
    own_input = lax.dynamic_slice_in_dim(rows_in, mdl_rank * row_dev, row_dev)
    own_residual = (own_input.astype(jnp.float32) + mixed_heads).astype(jnp.bfloat16)
    normed_ffn = rms_scale(own_residual, ffn_gain).astype(jnp.bfloat16)
    normed_ffn_all = gathered_over(normed_ffn, "mdl")

    gate_proj = jnp.dot(normed_ffn_all, w_shared_gate, preferred_element_type=jnp.float32)
    up_proj = jnp.dot(normed_ffn_all, w_shared_up, preferred_element_type=jnp.float32)
    shared_act = (jax.nn.silu(gate_proj) * up_proj).astype(jnp.bfloat16)
    shared_out = summed_over(
        jnp.dot(shared_act, w_shared_down, preferred_element_type=jnp.float32).astype(jnp.bfloat16),
        "mdl",
        arrival_order=True,
    )

    onehot = (expert_ids[:, None] == expert_labels[None, :]).astype(jnp.int32)
    earlier = jnp.cumsum(onehot, axis=0) - onehot
    slot_index = jnp.sum(earlier * onehot, axis=1)
    target = expert_ids * capacity + slot_index
    placing = (
        (slot_ids[:, None] == target[None, :])
        .astype(jnp.int32)
        .reshape(slot_total, row_dev, top_count)
    )
    placing = (
        jnp.sum(placing, axis=2)
        .astype(jnp.bfloat16)
        .reshape(n_wide, expert_dev, capacity, row_dev)
    )
    outgoing = jnp.einsum(
        "sjkr,rd->sjkd", placing, normed_ffn, preferred_element_type=jnp.float32
    ).astype(jnp.bfloat16)
    buffer = lax.all_to_all(outgoing, ("tok", "mdl"), split_axis=0, concat_axis=0, tiled=True)
    e_gate = jnp.einsum("sjkd,jdf->sjkf", buffer, w_expert_gate, preferred_element_type=jnp.float32)
    e_up = jnp.einsum("sjkd,jdf->sjkf", buffer, w_expert_up, preferred_element_type=jnp.float32)
    expert_act = (jax.nn.silu(e_gate) * e_up).astype(jnp.bfloat16)
    produced = jnp.einsum(
        "sjkf,jfd->sjkd", expert_act, w_expert_down, preferred_element_type=jnp.float32
    ).astype(jnp.bfloat16)
    returned = lax.all_to_all(produced, ("tok", "mdl"), split_axis=0, concat_axis=0, tiled=True)
    matched = target.reshape(row_dev, top_count)[:, :, None] == slot_ids[None, None, :]
    combining = jnp.sum(jnp.where(matched, weight_rows[:, :, None], 0.0), axis=1).reshape(
        row_dev, n_wide, expert_dev, capacity
    )
    routed = jnp.einsum(
        "rsjk,sjkd->rd",
        combining,
        returned.astype(jnp.float32),
        precision=lax.Precision.HIGHEST,
    )
    finished = (own_residual.astype(jnp.float32) + shared_out + routed).astype(jnp.bfloat16)
    return finished[None]


def solution(mesh):
    in_specs = (
        P(None, "tok", None),
        P(),
        P(None, ("tok", "mdl"), None),
        P(None, ("tok", "mdl"), None),
        P(),
        P(None, "mdl"),
        P(),
        P(),
        P(None, "mdl"),
        P("mdl", None),
        P(),
        P(None, "mdl"),
        P(None, "mdl"),
        P("mdl", None),
        P(("tok", "mdl"), None, None),
        P(("tok", "mdl"), None, None),
        P(("tok", "mdl"), None, None),
    )
    out_specs = P("section", ("tok", "mdl"), None)
    return jax.shard_map(shards, mesh=mesh, in_specs=in_specs, out_specs=out_specs, check_vma=False)
```

```python
import math

import jax
import jax.numpy as jnp
from jax import lax
from jax.sharding import PartitionSpec as P

NOPE = 128
ROPE = 64
VDIM = 128
LATENT = 512
SEGS = 4
LONGEST_SEGMENT = 1024


EPS = 1e-06


def passed_along(value, axis, steps):
    count = lax.axis_size(axis)
    initial, last = (max(0, -steps), min(count, count - steps))
    return lax.ppermute(value, axis, [(source, source + steps) for source in range(initial, last)])


def summed_over(parts, axis, arrival_order=False):
    count = lax.axis_size(axis)
    rank = lax.axis_index(axis)
    pieces = parts.reshape((count, parts.shape[0] // count) + parts.shape[1:])

    def piece_for(steps):
        if arrival_order:
            return pieces[(count - steps) % count]
        return lax.dynamic_index_in_dim(pieces, (rank + steps) % count, 0, keepdims=False)

    total = piece_for(0).astype(jnp.float32)
    for steps in range(1, count):
        moved = lax.ppermute(piece_for(steps), axis, [(i, (i + steps) % count) for i in range(count)])
        total = total + moved.astype(jnp.float32)
    return total


def gathered_over(block, axis):
    count = lax.axis_size(axis)
    arrived = [block]
    for steps in range(1, count):
        arrived.append(lax.ppermute(block, axis, [(i, (i + steps) % count) for i in range(count)]))
    return jnp.concatenate(arrived, axis=0)


def rms_scale(values, gain_vec):
    values = values.astype(jnp.float32)
    return values * lax.rsqrt(jnp.mean(values * values, axis=-1, keepdims=True) + EPS) * gain_vec


def rotary(values, positions):
    half_width = values.shape[-1] // 2
    frequency = 10000.0 ** (-jnp.arange(half_width, dtype=jnp.float32) / half_width)
    angles = positions.astype(jnp.float32)[:, None] * frequency[None, :]
    if values.ndim == 3:
        angles = angles[:, None, :]
    cosine = jnp.cos(angles)
    sine_part = jnp.sin(angles)
    lead_half = values[..., :half_width]
    tail_half = values[..., half_width:]
    return jnp.concatenate(
        [lead_half * cosine - tail_half * sine_part, lead_half * sine_part + tail_half * cosine],
        axis=-1,
    )


def positions_of(segment_row, segment_count):
    labels = jnp.arange(segment_count, dtype=jnp.int32)
    starts = jnp.sum((segment_row[None, :] < labels[:, None]).astype(jnp.int32), axis=1)
    member = (segment_row[:, None] == labels[None, :]).astype(jnp.int32)
    return jnp.arange(segment_row.shape[0], dtype=jnp.int32) - jnp.sum(
        member * starts[None, :], axis=1
    )


def shards(
    layer_input,
    segment_ids,
    route_ids,
    route_weights,
    attn_gain,
    w_query,
    w_kv_down,
    latent_gain,
    w_kv_up,
    w_out,
    ffn_gain,
    w_shared_gate,
    w_shared_up,
    w_shared_down,
    w_expert_gate,
    w_expert_up,
    w_expert_down,
):
    n_mdl = lax.axis_size("mdl")
    n_wide = lax.axis_size(("tok", "mdl"))
    section_id = lax.axis_index("section")
    tok_rank = lax.axis_index("tok")
    mdl_rank = lax.axis_index("mdl")
    micro_count, tok_dev, model_width = layer_input.shape
    row_dev = tok_dev // n_mdl
    top_count = route_ids.shape[2]
    local_heads = w_out.shape[0] // VDIM
    qk_width = NOPE + ROPE
    score_scale = 1.0 / math.sqrt(qk_width)
    expert_dev = w_expert_gate.shape[0]
    expert_total = expert_dev * n_wide
    capacity = max(2, 3 * row_dev * top_count // (2 * expert_total))
    slot_total = expert_total * capacity
    slot_ids = jnp.arange(slot_total, dtype=jnp.int32)
    expert_labels = jnp.arange(expert_total, dtype=jnp.int32)

    segment_row = lax.dynamic_index_in_dim(segment_ids, section_id, 0, keepdims=False)
    rows_in = lax.dynamic_index_in_dim(layer_input, section_id, 0, keepdims=False)
    expert_ids = lax.dynamic_index_in_dim(route_ids, section_id, 0, keepdims=False).reshape(-1)
    weight_rows = lax.dynamic_index_in_dim(route_weights, section_id, 0, keepdims=False)

    positions = positions_of(segment_row, SEGS)
    query_start = tok_rank * tok_dev
    query_pos = lax.dynamic_slice_in_dim(positions, query_start, tok_dev)
    query_seg = lax.dynamic_slice_in_dim(segment_row, query_start, tok_dev)
    query_index = query_start + jnp.arange(tok_dev, dtype=jnp.int32)

    normed = rms_scale(rows_in, attn_gain).astype(jnp.bfloat16)
    queries = jnp.dot(normed, w_query, preferred_element_type=jnp.float32).reshape(
        tok_dev, local_heads, qk_width
    )
    queries = jnp.concatenate(
        [queries[..., :NOPE], rotary(queries[..., NOPE:], query_pos)], axis=-1
    ).astype(jnp.bfloat16)
    compressed = jnp.dot(normed, w_kv_down, preferred_element_type=jnp.float32)
    latent = rms_scale(compressed[:, :LATENT], latent_gain).astype(jnp.bfloat16)
    key_rope = rotary(compressed[:, LATENT:], query_pos).astype(jnp.bfloat16)
    n_tok = lax.axis_size("tok")
    reach = LONGEST_SEGMENT // tok_dev
    kv_own = jnp.concatenate([latent, key_rope], axis=-1)
    kv_parts = [kv_own]
    for steps in range(1, min(reach, n_tok - 1) + 1):
        kv_parts.insert(0, passed_along(kv_own, "tok", steps))
    padded_seg = jnp.concatenate([jnp.full((tok_dev * len(kv_parts),), -1, jnp.int32), segment_row])

    def block_scores(kv_rows, first_key):
        key_count = kv_rows.shape[0]
        expanded = (
            jnp.dot(kv_rows[:, :LATENT], w_kv_up, preferred_element_type=jnp.float32)
            .astype(jnp.bfloat16)
            .reshape(key_count, local_heads, NOPE + VDIM)
        )
        scores = jnp.einsum(
            "qhd,khd->hqk", queries[..., :NOPE], expanded[..., :NOPE],
            preferred_element_type=jnp.float32,
        )
        scores = scores + jnp.einsum(
            "qhd,kd->hqk", queries[..., NOPE:], kv_rows[:, LATENT:],
            preferred_element_type=jnp.float32,
        )
        scores = scores * score_scale
        key_index = first_key + jnp.arange(key_count, dtype=jnp.int32)
        key_seg = lax.dynamic_slice_in_dim(padded_seg, first_key + padded_seg.shape[0] - segment_row.shape[0], key_count)
        allowed = (
            (key_seg[None, :] == query_seg[:, None])
            & (key_index[None, :] <= query_index[:, None])
            & (key_index[None, :] >= 0)
        )
        return scores, allowed[None, :, :], expanded[..., NOPE:]

    own_scores, own_allowed, own_values = block_scores(kv_own, query_start)
    running_max = jnp.max(jnp.where(own_allowed, own_scores, -1e30), axis=-1, keepdims=True)
    own_weights = jnp.where(own_allowed, jnp.exp(own_scores - running_max), 0.0)
    totals = jnp.sum(own_weights, axis=-1, keepdims=True)
    weighted = jnp.einsum(
        "hqk,khd->hqd", own_weights.astype(jnp.bfloat16), own_values,
        preferred_element_type=jnp.float32,
    )
    if len(kv_parts) > 1:
        earlier_rows = jnp.concatenate(kv_parts[:-1], axis=0)
        scores, allowed, values = block_scores(earlier_rows, query_start - earlier_rows.shape[0])
        new_max = jnp.maximum(
            running_max, jnp.max(jnp.where(allowed, scores, -1e30), axis=-1, keepdims=True)
        )
        weights = jnp.where(allowed, jnp.exp(scores - new_max), 0.0)
        factor = jnp.exp(running_max - new_max)
        totals = totals * factor + jnp.sum(weights, axis=-1, keepdims=True)
        weighted = weighted * factor + jnp.einsum(
            "hqk,khd->hqd", weights.astype(jnp.bfloat16), values,
            preferred_element_type=jnp.float32,
        )
    attended = (
        (weighted / totals).astype(jnp.bfloat16).transpose(1, 0, 2).reshape(tok_dev, local_heads * VDIM)
    )
    head_parts = jnp.dot(attended, w_out, preferred_element_type=jnp.float32).astype(jnp.bfloat16)
    mixed_heads = summed_over(head_parts, "mdl")
    own_input = lax.dynamic_slice_in_dim(rows_in, mdl_rank * row_dev, row_dev)
    own_residual = (own_input.astype(jnp.float32) + mixed_heads).astype(jnp.bfloat16)
    normed_ffn = rms_scale(own_residual, ffn_gain).astype(jnp.bfloat16)
    normed_ffn_all = gathered_over(normed_ffn, "mdl")

    gate_proj = jnp.dot(normed_ffn_all, w_shared_gate, preferred_element_type=jnp.float32)
    up_proj = jnp.dot(normed_ffn_all, w_shared_up, preferred_element_type=jnp.float32)
    shared_act = (jax.nn.silu(gate_proj) * up_proj).astype(jnp.bfloat16)
    shared_out = summed_over(
        jnp.dot(shared_act, w_shared_down, preferred_element_type=jnp.float32).astype(jnp.bfloat16),
        "mdl",
        arrival_order=True,
    )

    onehot = (expert_ids[:, None] == expert_labels[None, :]).astype(jnp.int32)
    earlier = jnp.cumsum(onehot, axis=0) - onehot
    slot_index = jnp.sum(earlier * onehot, axis=1)
    target = expert_ids * capacity + slot_index
    placing = (
        (slot_ids[:, None] == target[None, :])
        .astype(jnp.int32)
        .reshape(slot_total, row_dev, top_count)
    )
    placing = (
        jnp.sum(placing, axis=2)
        .astype(jnp.bfloat16)
        .reshape(n_wide, expert_dev, capacity, row_dev)
    )
    outgoing = jnp.einsum(
        "sjkr,rd->sjkd", placing, normed_ffn, preferred_element_type=jnp.float32
    ).astype(jnp.bfloat16)
    buffer = lax.all_to_all(outgoing, ("tok", "mdl"), split_axis=0, concat_axis=0, tiled=True)
    e_gate = jnp.einsum("sjkd,jdf->sjkf", buffer, w_expert_gate, preferred_element_type=jnp.float32)
    e_up = jnp.einsum("sjkd,jdf->sjkf", buffer, w_expert_up, preferred_element_type=jnp.float32)
    expert_act = (jax.nn.silu(e_gate) * e_up).astype(jnp.bfloat16)
    produced = jnp.einsum(
        "sjkf,jfd->sjkd", expert_act, w_expert_down, preferred_element_type=jnp.float32
    ).astype(jnp.bfloat16)
    returned = lax.all_to_all(produced, ("tok", "mdl"), split_axis=0, concat_axis=0, tiled=True)
    matched = target.reshape(row_dev, top_count)[:, :, None] == slot_ids[None, None, :]
    combining = jnp.sum(jnp.where(matched, weight_rows[:, :, None], 0.0), axis=1).reshape(
        row_dev, n_wide, expert_dev, capacity
    )
    routed = jnp.einsum(
        "rsjk,sjkd->rd",
        combining,
        returned.astype(jnp.float32),
        precision=lax.Precision.HIGH,
    )
    finished = (own_residual.astype(jnp.float32) + shared_out + routed).astype(jnp.bfloat16)
    return finished[None]


def solution(mesh):
    in_specs = (
        P(None, "tok", None),
        P(),
        P(None, ("tok", "mdl"), None),
        P(None, ("tok", "mdl"), None),
        P(),
        P(None, "mdl"),
        P(),
        P(),
        P(None, "mdl"),
        P("mdl", None),
        P(),
        P(None, "mdl"),
        P(None, "mdl"),
        P("mdl", None),
        P(("tok", "mdl"), None, None),
        P(("tok", "mdl"), None, None),
        P(("tok", "mdl"), None, None),
    )
    out_specs = P("section", ("tok", "mdl"), None)
    return jax.shard_map(shards, mesh=mesh, in_specs=in_specs, out_specs=out_specs, check_vma=False)
```

```python
import math

import jax
import jax.numpy as jnp
from jax import lax
from jax.sharding import PartitionSpec as P

NOPE = 128
ROPE = 64
VDIM = 128
LATENT = 512
SEGS = 4
LONGEST_SEGMENT = 1024


EPS = 1e-06


def passed_along(value, axis, steps):
    count = lax.axis_size(axis)
    initial, last = (max(0, -steps), min(count, count - steps))
    return lax.ppermute(value, axis, [(source, source + steps) for source in range(initial, last)])


def summed_over(parts, axis, arrival_order=False):
    count = lax.axis_size(axis)
    rank = lax.axis_index(axis)
    pieces = parts.reshape((count, parts.shape[0] // count) + parts.shape[1:])

    def pair_for(steps):
        if arrival_order:
            return pieces[2 * steps], pieces[2 * steps + 1]
        owner = (rank - 2 * steps) % count
        return (
            lax.dynamic_index_in_dim(pieces, owner, 0, keepdims=False),
            lax.dynamic_index_in_dim(pieces, owner ^ 1, 0, keepdims=False),
        )

    mine, partners = pair_for(0)
    mine = mine.astype(jnp.float32)
    partners = partners.astype(jnp.float32)
    for steps in range(1, count // 2):
        moved = lax.ppermute(
            jnp.stack(pair_for(steps)), axis, [(i, (i - 2 * steps) % count) for i in range(count)]
        )
        mine = mine + moved[0].astype(jnp.float32)
        partners = partners + moved[1].astype(jnp.float32)
    return mine + lax.ppermute(partners, axis, [(i, i ^ 1) for i in range(count)])


def gathered_over(block, axis):
    count = lax.axis_size(axis)
    pair = jnp.concatenate([block, lax.ppermute(block, axis, [(i, i ^ 1) for i in range(count)])])
    arrived = [pair]
    for steps in range(1, count // 2):
        arrived.append(lax.ppermute(pair, axis, [(i, (i + 2 * steps) % count) for i in range(count)]))
    return jnp.concatenate(arrived, axis=0)


def rms_scale(values, gain_vec):
    values = values.astype(jnp.float32)
    return values * lax.rsqrt(jnp.mean(values * values, axis=-1, keepdims=True) + EPS) * gain_vec


def rotary(values, positions):
    half_width = values.shape[-1] // 2
    frequency = 10000.0 ** (-jnp.arange(half_width, dtype=jnp.float32) / half_width)
    angles = positions.astype(jnp.float32)[:, None] * frequency[None, :]
    if values.ndim == 3:
        angles = angles[:, None, :]
    cosine = jnp.cos(angles)
    sine_part = jnp.sin(angles)
    lead_half = values[..., :half_width]
    tail_half = values[..., half_width:]
    return jnp.concatenate(
        [lead_half * cosine - tail_half * sine_part, lead_half * sine_part + tail_half * cosine],
        axis=-1,
    )


def positions_of(segment_row, segment_count):
    labels = jnp.arange(segment_count, dtype=jnp.int32)
    starts = jnp.sum((segment_row[None, :] < labels[:, None]).astype(jnp.int32), axis=1)
    member = (segment_row[:, None] == labels[None, :]).astype(jnp.int32)
    return jnp.arange(segment_row.shape[0], dtype=jnp.int32) - jnp.sum(
        member * starts[None, :], axis=1
    )


def shards(
    layer_input,
    segment_ids,
    route_ids,
    route_weights,
    attn_gain,
    w_query,
    w_kv_down,
    latent_gain,
    w_kv_up,
    w_out,
    ffn_gain,
    w_shared_gate,
    w_shared_up,
    w_shared_down,
    w_expert_gate,
    w_expert_up,
    w_expert_down,
):
    n_mdl = lax.axis_size("mdl")
    n_wide = lax.axis_size(("tok", "mdl"))
    section_id = lax.axis_index("section")
    tok_rank = lax.axis_index("tok")
    mdl_rank = lax.axis_index("mdl")
    micro_count, tok_dev, model_width = layer_input.shape
    row_dev = tok_dev // n_mdl
    top_count = route_ids.shape[2]
    local_heads = w_out.shape[0] // VDIM
    qk_width = NOPE + ROPE
    score_scale = 1.0 / math.sqrt(qk_width)
    expert_dev = w_expert_gate.shape[0]
    expert_total = expert_dev * n_wide
    capacity = max(2, 3 * row_dev * top_count // (2 * expert_total))
    slot_total = expert_total * capacity
    slot_ids = jnp.arange(slot_total, dtype=jnp.int32)
    expert_labels = jnp.arange(expert_total, dtype=jnp.int32)

    segment_row = lax.dynamic_index_in_dim(segment_ids, section_id, 0, keepdims=False)
    rows_in = lax.dynamic_index_in_dim(layer_input, section_id, 0, keepdims=False)
    expert_ids = lax.dynamic_index_in_dim(route_ids, section_id, 0, keepdims=False).reshape(-1)
    weight_rows = lax.dynamic_index_in_dim(route_weights, section_id, 0, keepdims=False)

    positions = positions_of(segment_row, SEGS)
    query_start = tok_rank * tok_dev
    query_pos = lax.dynamic_slice_in_dim(positions, query_start, tok_dev)
    query_seg = lax.dynamic_slice_in_dim(segment_row, query_start, tok_dev)
    query_index = query_start + jnp.arange(tok_dev, dtype=jnp.int32)

    normed = rms_scale(rows_in, attn_gain).astype(jnp.bfloat16)
    queries = jnp.dot(normed, w_query, preferred_element_type=jnp.float32).reshape(
        tok_dev, local_heads, qk_width
    )
    queries = jnp.concatenate(
        [queries[..., :NOPE], rotary(queries[..., NOPE:], query_pos)], axis=-1
    ).astype(jnp.bfloat16)
    compressed = jnp.dot(normed, w_kv_down, preferred_element_type=jnp.float32)
    latent = rms_scale(compressed[:, :LATENT], latent_gain).astype(jnp.bfloat16)
    key_rope = rotary(compressed[:, LATENT:], query_pos).astype(jnp.bfloat16)
    n_tok = lax.axis_size("tok")
    reach = LONGEST_SEGMENT // tok_dev
    kv_own = jnp.concatenate([latent, key_rope], axis=-1)
    kv_parts = [kv_own]
    for steps in range(1, min(reach, n_tok - 1) + 1):
        kv_parts.insert(0, passed_along(kv_own, "tok", steps))
    kv_rows = jnp.concatenate(kv_parts, axis=0)
    key_count = kv_rows.shape[0]
    key_start = query_start + tok_dev - key_count
    expanded = (
        jnp.dot(kv_rows[:, :LATENT], w_kv_up, preferred_element_type=jnp.float32)
        .astype(jnp.bfloat16)
        .reshape(key_count, local_heads, NOPE + VDIM)
    )
    rope_keys = kv_rows[:, LATENT:]
    scores = jnp.einsum(
        "qhd,khd->hqk", queries[..., :NOPE], expanded[..., :NOPE],
        preferred_element_type=jnp.float32,
    )
    scores = scores + jnp.einsum(
        "qhd,kd->hqk", queries[..., NOPE:], rope_keys, preferred_element_type=jnp.float32
    )
    scores = scores * score_scale
    key_index = key_start + jnp.arange(key_count, dtype=jnp.int32)
    padded_seg = jnp.concatenate([jnp.full((key_count,), -1, jnp.int32), segment_row])
    key_seg = lax.dynamic_slice_in_dim(padded_seg, key_start + key_count, key_count)
    allowed = (
        (key_seg[None, :] == query_seg[:, None])
        & (key_index[None, :] <= query_index[:, None])
        & (key_index[None, :] >= 0)
    )
    allowed = allowed[None, :, :]
    masked = jnp.where(allowed, scores, -1e30)
    row_max = jnp.max(masked, axis=-1, keepdims=True)
    weights = jnp.where(allowed, jnp.exp(scores - row_max), 0.0)
    totals = jnp.sum(weights, axis=-1, keepdims=True)
    weighted = jnp.einsum(
        "hqk,khd->hqd", weights.astype(jnp.bfloat16), expanded[..., NOPE:],
        preferred_element_type=jnp.float32,
    )
    attended = (
        (weighted / totals).astype(jnp.bfloat16).transpose(1, 0, 2).reshape(tok_dev, local_heads * VDIM)
    )
    head_parts = jnp.dot(attended, w_out, preferred_element_type=jnp.float32).astype(jnp.bfloat16)
    mixed_heads = summed_over(head_parts, "mdl")
    own_input = lax.dynamic_slice_in_dim(rows_in, mdl_rank * row_dev, row_dev)
    own_residual = (own_input.astype(jnp.float32) + mixed_heads).astype(jnp.bfloat16)
    normed_ffn = rms_scale(own_residual, ffn_gain).astype(jnp.bfloat16)
    normed_ffn_all = gathered_over(normed_ffn, "mdl")

    gate_proj = jnp.dot(normed_ffn_all, w_shared_gate, preferred_element_type=jnp.float32)
    up_proj = jnp.dot(normed_ffn_all, w_shared_up, preferred_element_type=jnp.float32)
    shared_act = (jax.nn.silu(gate_proj) * up_proj).astype(jnp.bfloat16)
    shared_out = summed_over(
        jnp.dot(shared_act, w_shared_down, preferred_element_type=jnp.float32).astype(jnp.bfloat16),
        "mdl",
        arrival_order=True,
    )

    onehot = (expert_ids[:, None] == expert_labels[None, :]).astype(jnp.int32)
    earlier = jnp.cumsum(onehot, axis=0) - onehot
    slot_index = jnp.sum(earlier * onehot, axis=1)
    target = expert_ids * capacity + slot_index
    placing = (
        (slot_ids[:, None] == target[None, :])
        .astype(jnp.int32)
        .reshape(slot_total, row_dev, top_count)
    )
    placing = (
        jnp.sum(placing, axis=2)
        .astype(jnp.bfloat16)
        .reshape(n_wide, expert_dev, capacity, row_dev)
    )
    outgoing = jnp.einsum(
        "sjkr,rd->sjkd", placing, normed_ffn, preferred_element_type=jnp.float32
    ).astype(jnp.bfloat16)
    buffer = lax.all_to_all(outgoing, ("tok", "mdl"), split_axis=0, concat_axis=0, tiled=True)
    e_gate = jnp.einsum("sjkd,jdf->sjkf", buffer, w_expert_gate, preferred_element_type=jnp.float32)
    e_up = jnp.einsum("sjkd,jdf->sjkf", buffer, w_expert_up, preferred_element_type=jnp.float32)
    expert_act = (jax.nn.silu(e_gate) * e_up).astype(jnp.bfloat16)
    produced = jnp.einsum(
        "sjkf,jfd->sjkd", expert_act, w_expert_down, preferred_element_type=jnp.float32
    ).astype(jnp.bfloat16)
    returned = lax.all_to_all(produced, ("tok", "mdl"), split_axis=0, concat_axis=0, tiled=True)
    matched = target.reshape(row_dev, top_count)[:, :, None] == slot_ids[None, None, :]
    combining = jnp.sum(jnp.where(matched, weight_rows[:, :, None], 0.0), axis=1).reshape(
        row_dev, n_wide, expert_dev, capacity
    )
    routed = jnp.einsum(
        "rsjk,sjkd->rd",
        combining,
        returned.astype(jnp.float32),
        precision=lax.Precision.HIGH,
    )
    finished = (own_residual.astype(jnp.float32) + shared_out + routed).astype(jnp.bfloat16)
    return finished[None]


def solution(mesh):
    in_specs = (
        P(None, "tok", None),
        P(),
        P(None, ("tok", "mdl"), None),
        P(None, ("tok", "mdl"), None),
        P(),
        P(None, "mdl"),
        P(),
        P(),
        P(None, "mdl"),
        P("mdl", None),
        P(),
        P(None, "mdl"),
        P(None, "mdl"),
        P("mdl", None),
        P(("tok", "mdl"), None, None),
        P(("tok", "mdl"), None, None),
        P(("tok", "mdl"), None, None),
    )
    out_specs = P("section", ("tok", "mdl"), None)
    return jax.shard_map(shards, mesh=mesh, in_specs=in_specs, out_specs=out_specs, check_vma=False)
```

```python
import math

import jax
import jax.numpy as jnp
from jax import lax
from jax.sharding import PartitionSpec as P

NOPE = 128
ROPE = 64
VDIM = 128
LATENT = 512
SEGS = 4
LONGEST_SEGMENT = 1024


EPS = 1e-06


def passed_along(value, axis, steps):
    count = lax.axis_size(axis)
    initial, last = (max(0, -steps), min(count, count - steps))
    return lax.ppermute(value, axis, [(source, source + steps) for source in range(initial, last)])


def summed_over(parts, axis, arrival_order=False):
    count = lax.axis_size(axis)
    rank = lax.axis_index(axis)
    pieces = parts.reshape((count, parts.shape[0] // count) + parts.shape[1:])

    def piece_for(steps):
        if arrival_order:
            return pieces[(count - steps) % count]
        return lax.dynamic_index_in_dim(pieces, (rank + steps) % count, 0, keepdims=False)

    total = piece_for(0).astype(jnp.float32)
    for steps in range(1, count):
        moved = lax.ppermute(piece_for(steps), axis, [(i, (i + steps) % count) for i in range(count)])
        total = total + moved.astype(jnp.float32)
    return total


def gathered_over(block, axis):
    count = lax.axis_size(axis)
    arrived = [block]
    for steps in range(1, count):
        arrived.append(lax.ppermute(block, axis, [(i, (i + steps) % count) for i in range(count)]))
    return jnp.concatenate(arrived, axis=0)


def rms_scale(values, gain_vec):
    values = values.astype(jnp.float32)
    return values * lax.rsqrt(jnp.mean(values * values, axis=-1, keepdims=True) + EPS) * gain_vec


def rotary(values, positions):
    half_width = values.shape[-1] // 2
    frequency = 10000.0 ** (-jnp.arange(half_width, dtype=jnp.float32) / half_width)
    angles = positions.astype(jnp.float32)[:, None] * frequency[None, :]
    if values.ndim == 3:
        angles = angles[:, None, :]
    cosine = jnp.cos(angles)
    sine_part = jnp.sin(angles)
    lead_half = values[..., :half_width]
    tail_half = values[..., half_width:]
    return jnp.concatenate(
        [lead_half * cosine - tail_half * sine_part, lead_half * sine_part + tail_half * cosine],
        axis=-1,
    )


def positions_of(segment_row, segment_count):
    labels = jnp.arange(segment_count, dtype=jnp.int32)
    starts = jnp.sum((segment_row[None, :] < labels[:, None]).astype(jnp.int32), axis=1)
    member = (segment_row[:, None] == labels[None, :]).astype(jnp.int32)
    return jnp.arange(segment_row.shape[0], dtype=jnp.int32) - jnp.sum(
        member * starts[None, :], axis=1
    )


def shards(
    layer_input,
    segment_ids,
    route_ids,
    route_weights,
    attn_gain,
    w_query,
    w_kv_down,
    latent_gain,
    w_kv_up,
    w_out,
    ffn_gain,
    w_shared_gate,
    w_shared_up,
    w_shared_down,
    w_expert_gate,
    w_expert_up,
    w_expert_down,
):
    n_mdl = lax.axis_size("mdl")
    n_wide = lax.axis_size(("tok", "mdl"))
    section_id = lax.axis_index("section")
    tok_rank = lax.axis_index("tok")
    mdl_rank = lax.axis_index("mdl")
    micro_count, tok_dev, model_width = layer_input.shape
    row_dev = tok_dev // n_mdl
    top_count = route_ids.shape[2]
    local_heads = w_out.shape[0] // VDIM
    qk_width = NOPE + ROPE
    score_scale = 1.0 / math.sqrt(qk_width)
    expert_dev = w_expert_gate.shape[0]
    expert_total = expert_dev * n_wide
    capacity = max(2, 3 * row_dev * top_count // (2 * expert_total))
    slot_total = expert_total * capacity
    slot_ids = jnp.arange(slot_total, dtype=jnp.int32)
    expert_labels = jnp.arange(expert_total, dtype=jnp.int32)

    segment_row = lax.dynamic_index_in_dim(segment_ids, section_id, 0, keepdims=False)
    rows_in = lax.dynamic_index_in_dim(layer_input, section_id, 0, keepdims=False)
    expert_ids = lax.dynamic_index_in_dim(route_ids, section_id, 0, keepdims=False).reshape(-1)
    weight_rows = lax.dynamic_index_in_dim(route_weights, section_id, 0, keepdims=False)

    positions = positions_of(segment_row, SEGS)
    query_start = tok_rank * tok_dev
    query_pos = lax.dynamic_slice_in_dim(positions, query_start, tok_dev)
    query_seg = lax.dynamic_slice_in_dim(segment_row, query_start, tok_dev)
    query_index = query_start + jnp.arange(tok_dev, dtype=jnp.int32)

    normed = rms_scale(rows_in, attn_gain).astype(jnp.bfloat16)
    queries = jnp.dot(normed, w_query, preferred_element_type=jnp.float32).reshape(
        tok_dev, local_heads, qk_width
    )
    queries = jnp.concatenate(
        [queries[..., :NOPE], rotary(queries[..., NOPE:], query_pos)], axis=-1
    ).astype(jnp.bfloat16)
    compressed = jnp.dot(normed, w_kv_down, preferred_element_type=jnp.float32)
    latent = rms_scale(compressed[:, :LATENT], latent_gain).astype(jnp.bfloat16)
    key_rope = rotary(compressed[:, LATENT:], query_pos).astype(jnp.bfloat16)
    n_tok = lax.axis_size("tok")
    reach = LONGEST_SEGMENT // tok_dev
    kv_own = jnp.concatenate([latent, key_rope], axis=-1)
    kv_parts = [kv_own]
    for steps in range(1, min(reach, n_tok - 1) + 1):
        kv_parts.insert(0, passed_along(kv_own, "tok", steps))
    kv_rows = jnp.concatenate(kv_parts, axis=0)
    key_count = kv_rows.shape[0]
    key_start = query_start + tok_dev - key_count
    expanded = (
        jnp.dot(kv_rows[:, :LATENT], w_kv_up, preferred_element_type=jnp.float32)
        .astype(jnp.bfloat16)
        .reshape(key_count, local_heads, NOPE + VDIM)
    )
    rope_keys = kv_rows[:, LATENT:]
    scores = jnp.einsum(
        "qhd,khd->hqk", queries[..., :NOPE], expanded[..., :NOPE],
        preferred_element_type=jnp.float32,
    )
    scores = scores + jnp.einsum(
        "qhd,kd->hqk", queries[..., NOPE:], rope_keys, preferred_element_type=jnp.float32
    )
    scores = scores * score_scale
    key_index = key_start + jnp.arange(key_count, dtype=jnp.int32)
    padded_seg = jnp.concatenate([jnp.full((key_count,), -1, jnp.int32), segment_row])
    key_seg = lax.dynamic_slice_in_dim(padded_seg, key_start + key_count, key_count)
    allowed = (
        (key_seg[None, :] == query_seg[:, None])
        & (key_index[None, :] <= query_index[:, None])
        & (key_index[None, :] >= 0)
    )
    allowed = allowed[None, :, :]
    masked = jnp.where(allowed, scores, -1e30)
    row_max = jnp.max(masked, axis=-1, keepdims=True)
    weights = jnp.where(allowed, jnp.exp(scores - row_max), 0.0)
    totals = jnp.sum(weights, axis=-1, keepdims=True)
    weighted = jnp.einsum(
        "hqk,khd->hqd", weights.astype(jnp.bfloat16), expanded[..., NOPE:],
        preferred_element_type=jnp.float32,
    )
    attended = (
        (weighted / totals).astype(jnp.bfloat16).transpose(1, 0, 2).reshape(tok_dev, local_heads * VDIM)
    )
    head_parts = jnp.dot(attended, w_out, preferred_element_type=jnp.float32).astype(jnp.bfloat16)
    mixed_heads = summed_over(head_parts, "mdl")
    own_input = lax.dynamic_slice_in_dim(rows_in, mdl_rank * row_dev, row_dev)
    own_residual = (own_input.astype(jnp.float32) + mixed_heads).astype(jnp.bfloat16)
    normed_ffn = rms_scale(own_residual, ffn_gain).astype(jnp.bfloat16)
    normed_ffn_all = gathered_over(normed_ffn, "mdl")

    gate_proj = jnp.dot(normed_ffn_all, w_shared_gate, preferred_element_type=jnp.float32)
    up_proj = jnp.dot(normed_ffn_all, w_shared_up, preferred_element_type=jnp.float32)
    shared_act = (jax.nn.silu(gate_proj) * up_proj).astype(jnp.bfloat16)
    shared_out = summed_over(
        jnp.dot(shared_act, w_shared_down, preferred_element_type=jnp.float32).astype(jnp.bfloat16),
        "mdl",
        arrival_order=True,
    )

    onehot = (expert_ids[:, None] == expert_labels[None, :]).astype(jnp.int32)
    earlier = jnp.cumsum(onehot, axis=0) - onehot
    slot_index = jnp.sum(earlier * onehot, axis=1)
    target = expert_ids * capacity + slot_index
    placing = (
        (slot_ids[:, None] == target[None, :])
        .astype(jnp.int32)
        .reshape(slot_total, row_dev, top_count)
    )
    placing = (
        jnp.sum(placing, axis=2)
        .astype(jnp.bfloat16)
        .reshape(n_wide, expert_dev, capacity, row_dev)
    )
    outgoing = jnp.einsum(
        "sjkr,rd->sjkd", placing, normed_ffn, preferred_element_type=jnp.float32
    ).astype(jnp.bfloat16)
    buffer = lax.all_to_all(outgoing, ("tok", "mdl"), split_axis=0, concat_axis=0, tiled=True)
    e_gate = jnp.einsum("sjkd,jdf->sjkf", buffer, w_expert_gate, preferred_element_type=jnp.float32)
    e_up = jnp.einsum("sjkd,jdf->sjkf", buffer, w_expert_up, preferred_element_type=jnp.float32)
    expert_act = (jax.nn.silu(e_gate) * e_up).astype(jnp.bfloat16)
    produced = jnp.einsum(
        "sjkf,jfd->sjkd", expert_act, w_expert_down, preferred_element_type=jnp.float32
    ).astype(jnp.bfloat16)
    returned = lax.all_to_all(produced, ("tok", "mdl"), split_axis=0, concat_axis=0, tiled=True)
    matched = target.reshape(row_dev, top_count)[:, :, None] == slot_ids[None, None, :]
    combining = jnp.sum(jnp.where(matched, weight_rows[:, :, None], 0.0), axis=1).reshape(
        row_dev, n_wide, expert_dev, capacity
    )
    weight_high = combining.astype(jnp.bfloat16)
    weight_low = (combining - weight_high.astype(jnp.float32)).astype(jnp.bfloat16)
    both_parts = jnp.einsum(
        "prsjk,sjkd->prd",
        jnp.stack([weight_high, weight_low]),
        returned,
        preferred_element_type=jnp.float32,
    )
    routed = both_parts[0] + both_parts[1]
    finished = (own_residual.astype(jnp.float32) + shared_out + routed).astype(jnp.bfloat16)
    return finished[None]


def solution(mesh):
    in_specs = (
        P(None, "tok", None),
        P(),
        P(None, ("tok", "mdl"), None),
        P(None, ("tok", "mdl"), None),
        P(),
        P(None, "mdl"),
        P(),
        P(),
        P(None, "mdl"),
        P("mdl", None),
        P(),
        P(None, "mdl"),
        P(None, "mdl"),
        P("mdl", None),
        P(("tok", "mdl"), None, None),
        P(("tok", "mdl"), None, None),
        P(("tok", "mdl"), None, None),
    )
    out_specs = P("section", ("tok", "mdl"), None)
    return jax.shard_map(shards, mesh=mesh, in_specs=in_specs, out_specs=out_specs, check_vma=False)
```

```python
import math

import jax
import jax.numpy as jnp
from jax import lax
from jax.sharding import PartitionSpec as P

NOPE = 128
ROPE = 64
VDIM = 128
LATENT = 512
SEGS = 4
LONGEST_SEGMENT = 1024


EPS = 1e-06


def passed_along(value, axis, steps):
    count = lax.axis_size(axis)
    initial, last = (max(0, -steps), min(count, count - steps))
    return lax.ppermute(value, axis, [(source, source + steps) for source in range(initial, last)])


def summed_over(parts, axis, arrival_order=False):
    count = lax.axis_size(axis)
    rank = lax.axis_index(axis)
    pieces = parts.reshape((count, parts.shape[0] // count) + parts.shape[1:])

    def piece_for(steps):
        if arrival_order:
            return pieces[(count - steps) % count]
        return lax.dynamic_index_in_dim(pieces, (rank + steps) % count, 0, keepdims=False)

    total = piece_for(0).astype(jnp.float32)
    for steps in range(1, count):
        moved = lax.ppermute(piece_for(steps), axis, [(i, (i + steps) % count) for i in range(count)])
        total = total + moved.astype(jnp.float32)
    return total


def gathered_over(block, axis):
    count = lax.axis_size(axis)
    arrived = [block]
    for steps in range(1, count):
        arrived.append(lax.ppermute(block, axis, [(i, (i + steps) % count) for i in range(count)]))
    return jnp.concatenate(arrived, axis=0)


def rms_scale(values, gain_vec):
    values = values.astype(jnp.float32)
    return values * lax.rsqrt(jnp.mean(values * values, axis=-1, keepdims=True) + EPS) * gain_vec


def rotary(values, positions):
    half_width = values.shape[-1] // 2
    frequency = 10000.0 ** (-jnp.arange(half_width, dtype=jnp.float32) / half_width)
    angles = positions.astype(jnp.float32)[:, None] * frequency[None, :]
    if values.ndim == 3:
        angles = angles[:, None, :]
    cosine = jnp.cos(angles)
    sine_part = jnp.sin(angles)
    lead_half = values[..., :half_width]
    tail_half = values[..., half_width:]
    return jnp.concatenate(
        [lead_half * cosine - tail_half * sine_part, lead_half * sine_part + tail_half * cosine],
        axis=-1,
    )


def positions_of(segment_row, segment_count):
    labels = jnp.arange(segment_count, dtype=jnp.int32)
    starts = jnp.sum((segment_row[None, :] < labels[:, None]).astype(jnp.int32), axis=1)
    member = (segment_row[:, None] == labels[None, :]).astype(jnp.int32)
    return jnp.arange(segment_row.shape[0], dtype=jnp.int32) - jnp.sum(
        member * starts[None, :], axis=1
    )


def shards(
    layer_input,
    segment_ids,
    route_ids,
    route_weights,
    attn_gain,
    w_query,
    w_kv_down,
    latent_gain,
    w_kv_up,
    w_out,
    ffn_gain,
    w_shared_gate,
    w_shared_up,
    w_shared_down,
    w_expert_gate,
    w_expert_up,
    w_expert_down,
):
    n_mdl = lax.axis_size("mdl")
    n_wide = lax.axis_size(("tok", "mdl"))
    section_id = lax.axis_index("section")
    tok_rank = lax.axis_index("tok")
    mdl_rank = lax.axis_index("mdl")
    micro_count, tok_dev, model_width = layer_input.shape
    row_dev = tok_dev // n_mdl
    top_count = route_ids.shape[2]
    local_heads = w_out.shape[0] // VDIM
    qk_width = NOPE + ROPE
    score_scale = 1.0 / math.sqrt(qk_width)
    expert_dev = w_expert_gate.shape[0]
    expert_total = expert_dev * n_wide
    capacity = max(2, 3 * row_dev * top_count // (2 * expert_total))
    slot_total = expert_total * capacity
    slot_ids = jnp.arange(slot_total, dtype=jnp.int32)
    expert_labels = jnp.arange(expert_total, dtype=jnp.int32)

    segment_row = lax.dynamic_index_in_dim(segment_ids, section_id, 0, keepdims=False)
    rows_in = lax.dynamic_index_in_dim(layer_input, section_id, 0, keepdims=False)
    expert_ids = lax.dynamic_index_in_dim(route_ids, section_id, 0, keepdims=False).reshape(-1)
    weight_rows = lax.dynamic_index_in_dim(route_weights, section_id, 0, keepdims=False)

    positions = positions_of(segment_row, SEGS)
    query_start = tok_rank * tok_dev
    query_pos = lax.dynamic_slice_in_dim(positions, query_start, tok_dev)
    query_seg = lax.dynamic_slice_in_dim(segment_row, query_start, tok_dev)
    query_index = query_start + jnp.arange(tok_dev, dtype=jnp.int32)

    normed = rms_scale(rows_in, attn_gain).astype(jnp.bfloat16)
    queries = jnp.dot(normed, w_query, preferred_element_type=jnp.float32).reshape(
        tok_dev, local_heads, qk_width
    )
    queries = jnp.concatenate(
        [queries[..., :NOPE], rotary(queries[..., NOPE:], query_pos)], axis=-1
    ).astype(jnp.bfloat16)
    compressed = jnp.dot(normed, w_kv_down, preferred_element_type=jnp.float32)
    latent = rms_scale(compressed[:, :LATENT], latent_gain).astype(jnp.bfloat16)
    key_rope = rotary(compressed[:, LATENT:], query_pos).astype(jnp.bfloat16)
    n_tok = lax.axis_size("tok")
    reach = LONGEST_SEGMENT // tok_dev
    kv_own = jnp.concatenate([latent, key_rope], axis=-1)
    kv_parts = [kv_own]
    if n_tok == 2 * reach:
        across = passed_along(kv_own, "tok", reach)
        place = tok_rank % reach
        for steps in range(1, reach):
            wraps = place + steps >= reach
            sent = jnp.where(wraps, across, kv_own)
            pairs = [
                (half * reach + i, half * reach + (i + steps) % reach)
                for half in range(2)
                for i in range(reach)
            ]
            kv_parts.insert(0, lax.ppermute(sent, "tok", pairs))
        kv_parts.insert(0, across)
    else:
        for steps in range(1, min(reach, n_tok - 1) + 1):
            kv_parts.insert(0, passed_along(kv_own, "tok", steps))
    kv_rows = jnp.concatenate(kv_parts, axis=0)
    key_count = kv_rows.shape[0]
    key_start = query_start + tok_dev - key_count
    expanded = (
        jnp.dot(kv_rows[:, :LATENT], w_kv_up, preferred_element_type=jnp.float32)
        .astype(jnp.bfloat16)
        .reshape(key_count, local_heads, NOPE + VDIM)
    )
    rope_keys = kv_rows[:, LATENT:]
    scores = jnp.einsum(
        "qhd,khd->hqk", queries[..., :NOPE], expanded[..., :NOPE],
        preferred_element_type=jnp.float32,
    )
    scores = scores + jnp.einsum(
        "qhd,kd->hqk", queries[..., NOPE:], rope_keys, preferred_element_type=jnp.float32
    )
    scores = scores * score_scale
    key_index = key_start + jnp.arange(key_count, dtype=jnp.int32)
    padded_seg = jnp.concatenate([jnp.full((key_count,), -1, jnp.int32), segment_row])
    key_seg = lax.dynamic_slice_in_dim(padded_seg, key_start + key_count, key_count)
    allowed = (
        (key_seg[None, :] == query_seg[:, None])
        & (key_index[None, :] <= query_index[:, None])
        & (key_index[None, :] >= 0)
    )
    allowed = allowed[None, :, :]
    masked = jnp.where(allowed, scores, -1e30)
    row_max = jnp.max(masked, axis=-1, keepdims=True)
    weights = jnp.where(allowed, jnp.exp(scores - row_max), 0.0)
    totals = jnp.sum(weights, axis=-1, keepdims=True)
    weighted = jnp.einsum(
        "hqk,khd->hqd", weights.astype(jnp.bfloat16), expanded[..., NOPE:],
        preferred_element_type=jnp.float32,
    )
    attended = (
        (weighted / totals).astype(jnp.bfloat16).transpose(1, 0, 2).reshape(tok_dev, local_heads * VDIM)
    )
    head_parts = jnp.dot(attended, w_out, preferred_element_type=jnp.float32).astype(jnp.bfloat16)
    mixed_heads = summed_over(head_parts, "mdl")
    own_input = lax.dynamic_slice_in_dim(rows_in, mdl_rank * row_dev, row_dev)
    own_residual = (own_input.astype(jnp.float32) + mixed_heads).astype(jnp.bfloat16)
    normed_ffn = rms_scale(own_residual, ffn_gain).astype(jnp.bfloat16)
    normed_ffn_all = gathered_over(normed_ffn, "mdl")

    gate_proj = jnp.dot(normed_ffn_all, w_shared_gate, preferred_element_type=jnp.float32)
    up_proj = jnp.dot(normed_ffn_all, w_shared_up, preferred_element_type=jnp.float32)
    shared_act = (jax.nn.silu(gate_proj) * up_proj).astype(jnp.bfloat16)
    shared_out = summed_over(
        jnp.dot(shared_act, w_shared_down, preferred_element_type=jnp.float32).astype(jnp.bfloat16),
        "mdl",
        arrival_order=True,
    )

    onehot = (expert_ids[:, None] == expert_labels[None, :]).astype(jnp.int32)
    earlier = jnp.cumsum(onehot, axis=0) - onehot
    slot_index = jnp.sum(earlier * onehot, axis=1)
    target = expert_ids * capacity + slot_index
    placing = (
        (slot_ids[:, None] == target[None, :])
        .astype(jnp.int32)
        .reshape(slot_total, row_dev, top_count)
    )
    placing = (
        jnp.sum(placing, axis=2)
        .astype(jnp.bfloat16)
        .reshape(n_wide, expert_dev, capacity, row_dev)
    )
    outgoing = jnp.einsum(
        "sjkr,rd->sjkd", placing, normed_ffn, preferred_element_type=jnp.float32
    ).astype(jnp.bfloat16)
    buffer = lax.all_to_all(outgoing, ("tok", "mdl"), split_axis=0, concat_axis=0, tiled=True)
    e_gate = jnp.einsum("sjkd,jdf->sjkf", buffer, w_expert_gate, preferred_element_type=jnp.float32)
    e_up = jnp.einsum("sjkd,jdf->sjkf", buffer, w_expert_up, preferred_element_type=jnp.float32)
    expert_act = (jax.nn.silu(e_gate) * e_up).astype(jnp.bfloat16)
    produced = jnp.einsum(
        "sjkf,jfd->sjkd", expert_act, w_expert_down, preferred_element_type=jnp.float32
    ).astype(jnp.bfloat16)
    returned = lax.all_to_all(produced, ("tok", "mdl"), split_axis=0, concat_axis=0, tiled=True)
    matched = target.reshape(row_dev, top_count)[:, :, None] == slot_ids[None, None, :]
    combining = jnp.sum(jnp.where(matched, weight_rows[:, :, None], 0.0), axis=1).reshape(
        row_dev, n_wide, expert_dev, capacity
    )
    routed = jnp.einsum(
        "rsjk,sjkd->rd",
        combining,
        returned.astype(jnp.float32),
        precision=lax.Precision.HIGHEST,
    )
    finished = (own_residual.astype(jnp.float32) + shared_out + routed).astype(jnp.bfloat16)
    return finished[None]


def solution(mesh):
    in_specs = (
        P(None, "tok", None),
        P(),
        P(None, ("tok", "mdl"), None),
        P(None, ("tok", "mdl"), None),
        P(),
        P(None, "mdl"),
        P(),
        P(),
        P(None, "mdl"),
        P("mdl", None),
        P(),
        P(None, "mdl"),
        P(None, "mdl"),
        P("mdl", None),
        P(("tok", "mdl"), None, None),
        P(("tok", "mdl"), None, None),
        P(("tok", "mdl"), None, None),
    )
    out_specs = P("section", ("tok", "mdl"), None)
    return jax.shard_map(shards, mesh=mesh, in_specs=in_specs, out_specs=out_specs, check_vma=False)
```

```python
import math

import jax
import jax.numpy as jnp
from jax import lax
from jax.sharding import PartitionSpec as P

NOPE = 128
ROPE = 64
VDIM = 128
LATENT = 512
SEGS = 4
LONGEST_SEGMENT = 1024


EPS = 1e-06


def passed_along(value, axis, steps):
    count = lax.axis_size(axis)
    initial, last = (max(0, -steps), min(count, count - steps))
    return lax.ppermute(value, axis, [(source, source + steps) for source in range(initial, last)])


def summed_over(parts, axis, arrival_order=False):
    count = lax.axis_size(axis)
    rank = lax.axis_index(axis)
    pieces = parts.reshape((count, parts.shape[0] // count) + parts.shape[1:])

    def piece_for(steps):
        if arrival_order:
            return pieces[(count - steps) % count]
        return lax.dynamic_index_in_dim(pieces, (rank + steps) % count, 0, keepdims=False)

    total = piece_for(0).astype(jnp.float32)
    for steps in range(1, count):
        moved = lax.ppermute(piece_for(steps), axis, [(i, (i + steps) % count) for i in range(count)])
        total = total + moved.astype(jnp.float32)
    return total


def gathered_over(block, axis):
    count = lax.axis_size(axis)
    arrived = [block]
    for steps in range(1, count):
        arrived.append(lax.ppermute(block, axis, [(i, (i + steps) % count) for i in range(count)]))
    return jnp.concatenate(arrived, axis=0)


def rms_scale(values, gain_vec):
    values = values.astype(jnp.float32)
    return values * lax.rsqrt(jnp.mean(values * values, axis=-1, keepdims=True) + EPS) * gain_vec


def rotary(values, positions):
    half_width = values.shape[-1] // 2
    frequency = 10000.0 ** (-jnp.arange(half_width, dtype=jnp.float32) / half_width)
    angles = positions.astype(jnp.float32)[:, None] * frequency[None, :]
    if values.ndim == 3:
        angles = angles[:, None, :]
    cosine = jnp.cos(angles)
    sine_part = jnp.sin(angles)
    lead_half = values[..., :half_width]
    tail_half = values[..., half_width:]
    return jnp.concatenate(
        [lead_half * cosine - tail_half * sine_part, lead_half * sine_part + tail_half * cosine],
        axis=-1,
    )


def positions_of(segment_row, segment_count):
    labels = jnp.arange(segment_count, dtype=jnp.int32)
    starts = jnp.sum((segment_row[None, :] < labels[:, None]).astype(jnp.int32), axis=1)
    member = (segment_row[:, None] == labels[None, :]).astype(jnp.int32)
    return jnp.arange(segment_row.shape[0], dtype=jnp.int32) - jnp.sum(
        member * starts[None, :], axis=1
    )


def shards(
    layer_input,
    segment_ids,
    route_ids,
    route_weights,
    attn_gain,
    w_query,
    w_kv_down,
    latent_gain,
    w_kv_up,
    w_out,
    ffn_gain,
    w_shared_gate,
    w_shared_up,
    w_shared_down,
    w_expert_gate,
    w_expert_up,
    w_expert_down,
):
    n_mdl = lax.axis_size("mdl")
    n_wide = lax.axis_size(("tok", "mdl"))
    section_id = lax.axis_index("section")
    tok_rank = lax.axis_index("tok")
    mdl_rank = lax.axis_index("mdl")
    micro_count, tok_dev, model_width = layer_input.shape
    row_dev = tok_dev // n_mdl
    top_count = route_ids.shape[2]
    local_heads = w_out.shape[0] // VDIM
    qk_width = NOPE + ROPE
    score_scale = 1.0 / math.sqrt(qk_width)
    expert_dev = w_expert_gate.shape[0]
    expert_total = expert_dev * n_wide
    capacity = max(2, 3 * row_dev * top_count // (2 * expert_total))
    slot_total = expert_total * capacity
    slot_ids = jnp.arange(slot_total, dtype=jnp.int32)
    expert_labels = jnp.arange(expert_total, dtype=jnp.int32)

    segment_row = lax.dynamic_index_in_dim(segment_ids, section_id, 0, keepdims=False)
    rows_in = lax.dynamic_index_in_dim(layer_input, section_id, 0, keepdims=False)
    expert_ids = lax.dynamic_index_in_dim(route_ids, section_id, 0, keepdims=False).reshape(-1)
    weight_rows = lax.dynamic_index_in_dim(route_weights, section_id, 0, keepdims=False)

    positions = positions_of(segment_row, SEGS)
    query_start = tok_rank * tok_dev
    query_pos = lax.dynamic_slice_in_dim(positions, query_start, tok_dev)
    query_seg = lax.dynamic_slice_in_dim(segment_row, query_start, tok_dev)
    query_index = query_start + jnp.arange(tok_dev, dtype=jnp.int32)

    normed = rms_scale(rows_in, attn_gain).astype(jnp.bfloat16)
    queries = jnp.dot(normed, w_query, preferred_element_type=jnp.float32).reshape(
        tok_dev, local_heads, qk_width
    )
    queries = jnp.concatenate(
        [queries[..., :NOPE], rotary(queries[..., NOPE:], query_pos)], axis=-1
    ).astype(jnp.bfloat16)
    compressed = jnp.dot(normed, w_kv_down, preferred_element_type=jnp.float32)
    latent = rms_scale(compressed[:, :LATENT], latent_gain).astype(jnp.bfloat16)
    key_rope = rotary(compressed[:, LATENT:], query_pos).astype(jnp.bfloat16)
    n_tok = lax.axis_size("tok")
    reach = LONGEST_SEGMENT // tok_dev
    kv_own = jnp.concatenate([latent, key_rope], axis=-1)
    kv_parts = [kv_own]
    if micro_count == 2 and lax.axis_size("section") == 2:
        other_id = 1 - section_id
        other_rows = lax.dynamic_index_in_dim(layer_input, other_id, 0, keepdims=False)
        other_seg = lax.dynamic_index_in_dim(segment_ids, other_id, 0, keepdims=False)
        other_pos = lax.dynamic_slice_in_dim(positions_of(other_seg, SEGS), query_start, tok_dev)
        other_normed = rms_scale(other_rows, attn_gain).astype(jnp.bfloat16)
        other_compressed = jnp.dot(other_normed, w_kv_down, preferred_element_type=jnp.float32)
        kv_other = jnp.concatenate(
            [
                rms_scale(other_compressed[:, :LATENT], latent_gain).astype(jnp.bfloat16),
                rotary(other_compressed[:, LATENT:], other_pos).astype(jnp.bfloat16),
            ],
            axis=-1,
        )
        half = n_tok // 2
        for steps in range(1, min(reach, n_tok - 1) + 1):
            crossing = (tok_rank < half) & (tok_rank + steps >= half)
            sent = jnp.where(crossing, kv_other, kv_own)
            pairs = []
            for sec in range(2):
                for t in range(n_tok - steps):
                    source = (1 - sec) if t < half <= t + steps else sec
                    pairs.append((source * n_tok + t, sec * n_tok + t + steps))
            kv_parts.insert(0, lax.ppermute(sent, ("section", "tok"), pairs))
    else:
        for steps in range(1, min(reach, n_tok - 1) + 1):
            kv_parts.insert(0, passed_along(kv_own, "tok", steps))
    kv_rows = jnp.concatenate(kv_parts, axis=0)
    key_count = kv_rows.shape[0]
    key_start = query_start + tok_dev - key_count
    expanded = (
        jnp.dot(kv_rows[:, :LATENT], w_kv_up, preferred_element_type=jnp.float32)
        .astype(jnp.bfloat16)
        .reshape(key_count, local_heads, NOPE + VDIM)
    )
    rope_keys = kv_rows[:, LATENT:]
    scores = jnp.einsum(
        "qhd,khd->hqk", queries[..., :NOPE], expanded[..., :NOPE],
        preferred_element_type=jnp.float32,
    )
    scores = scores + jnp.einsum(
        "qhd,kd->hqk", queries[..., NOPE:], rope_keys, preferred_element_type=jnp.float32
    )
    scores = scores * score_scale
    key_index = key_start + jnp.arange(key_count, dtype=jnp.int32)
    padded_seg = jnp.concatenate([jnp.full((key_count,), -1, jnp.int32), segment_row])
    key_seg = lax.dynamic_slice_in_dim(padded_seg, key_start + key_count, key_count)
    allowed = (
        (key_seg[None, :] == query_seg[:, None])
        & (key_index[None, :] <= query_index[:, None])
        & (key_index[None, :] >= 0)
    )
    allowed = allowed[None, :, :]
    masked = jnp.where(allowed, scores, -1e30)
    row_max = jnp.max(masked, axis=-1, keepdims=True)
    weights = jnp.where(allowed, jnp.exp(scores - row_max), 0.0)
    totals = jnp.sum(weights, axis=-1, keepdims=True)
    weighted = jnp.einsum(
        "hqk,khd->hqd", weights.astype(jnp.bfloat16), expanded[..., NOPE:],
        preferred_element_type=jnp.float32,
    )
    attended = (
        (weighted / totals).astype(jnp.bfloat16).transpose(1, 0, 2).reshape(tok_dev, local_heads * VDIM)
    )
    head_parts = jnp.dot(attended, w_out, preferred_element_type=jnp.float32).astype(jnp.bfloat16)
    mixed_heads = summed_over(head_parts, "mdl")
    own_input = lax.dynamic_slice_in_dim(rows_in, mdl_rank * row_dev, row_dev)
    own_residual = (own_input.astype(jnp.float32) + mixed_heads).astype(jnp.bfloat16)
    normed_ffn = rms_scale(own_residual, ffn_gain).astype(jnp.bfloat16)
    normed_ffn_all = gathered_over(normed_ffn, "mdl")

    gate_proj = jnp.dot(normed_ffn_all, w_shared_gate, preferred_element_type=jnp.float32)
    up_proj = jnp.dot(normed_ffn_all, w_shared_up, preferred_element_type=jnp.float32)
    shared_act = (jax.nn.silu(gate_proj) * up_proj).astype(jnp.bfloat16)
    shared_out = summed_over(
        jnp.dot(shared_act, w_shared_down, preferred_element_type=jnp.float32).astype(jnp.bfloat16),
        "mdl",
        arrival_order=True,
    )

    onehot = (expert_ids[:, None] == expert_labels[None, :]).astype(jnp.int32)
    earlier = jnp.cumsum(onehot, axis=0) - onehot
    slot_index = jnp.sum(earlier * onehot, axis=1)
    target = expert_ids * capacity + slot_index
    placing = (
        (slot_ids[:, None] == target[None, :])
        .astype(jnp.int32)
        .reshape(slot_total, row_dev, top_count)
    )
    placing = (
        jnp.sum(placing, axis=2)
        .astype(jnp.bfloat16)
        .reshape(n_wide, expert_dev, capacity, row_dev)
    )
    outgoing = jnp.einsum(
        "sjkr,rd->sjkd", placing, normed_ffn, preferred_element_type=jnp.float32
    ).astype(jnp.bfloat16)
    buffer = lax.all_to_all(outgoing, ("tok", "mdl"), split_axis=0, concat_axis=0, tiled=True)
    e_gate = jnp.einsum("sjkd,jdf->sjkf", buffer, w_expert_gate, preferred_element_type=jnp.float32)
    e_up = jnp.einsum("sjkd,jdf->sjkf", buffer, w_expert_up, preferred_element_type=jnp.float32)
    expert_act = (jax.nn.silu(e_gate) * e_up).astype(jnp.bfloat16)
    produced = jnp.einsum(
        "sjkf,jfd->sjkd", expert_act, w_expert_down, preferred_element_type=jnp.float32
    ).astype(jnp.bfloat16)
    returned = lax.all_to_all(produced, ("tok", "mdl"), split_axis=0, concat_axis=0, tiled=True)
    matched = target.reshape(row_dev, top_count)[:, :, None] == slot_ids[None, None, :]
    combining = jnp.sum(jnp.where(matched, weight_rows[:, :, None], 0.0), axis=1).reshape(
        row_dev, n_wide, expert_dev, capacity
    )
    routed = jnp.einsum(
        "rsjk,sjkd->rd",
        combining,
        returned.astype(jnp.float32),
        precision=lax.Precision.HIGHEST,
    )
    finished = (own_residual.astype(jnp.float32) + shared_out + routed).astype(jnp.bfloat16)
    return finished[None]


def solution(mesh):
    in_specs = (
        P(None, "tok", None),
        P(),
        P(None, ("tok", "mdl"), None),
        P(None, ("tok", "mdl"), None),
        P(),
        P(None, "mdl"),
        P(),
        P(),
        P(None, "mdl"),
        P("mdl", None),
        P(),
        P(None, "mdl"),
        P(None, "mdl"),
        P("mdl", None),
        P(("tok", "mdl"), None, None),
        P(("tok", "mdl"), None, None),
        P(("tok", "mdl"), None, None),
    )
    out_specs = P("section", ("tok", "mdl"), None)
    return jax.shard_map(shards, mesh=mesh, in_specs=in_specs, out_specs=out_specs, check_vma=False)
```

```python
import math

import jax
import jax.numpy as jnp
from jax import lax
from jax.sharding import PartitionSpec as P

NOPE = 128
ROPE = 64
VDIM = 128
LATENT = 512
SEGS = 4
LONGEST_SEGMENT = 1024


EPS = 1e-06


def passed_along(value, axis, steps):
    count = lax.axis_size(axis)
    initial, last = (max(0, -steps), min(count, count - steps))
    return lax.ppermute(value, axis, [(source, source + steps) for source in range(initial, last)])


def summed_over(parts, axis, arrival_order=False):
    count = lax.axis_size(axis)
    rank = lax.axis_index(axis)
    pieces = parts.reshape((count, parts.shape[0] // count) + parts.shape[1:])

    def piece_for(steps):
        if arrival_order:
            return pieces[(count - steps) % count]
        return lax.dynamic_index_in_dim(pieces, (rank + steps) % count, 0, keepdims=False)

    total = piece_for(0).astype(jnp.float32)
    for steps in range(1, count):
        moved = lax.ppermute(piece_for(steps), axis, [(i, (i + steps) % count) for i in range(count)])
        total = total + moved.astype(jnp.float32)
    return total


def gathered_over(block, axis):
    count = lax.axis_size(axis)
    arrived = [block]
    for steps in range(1, count):
        arrived.append(lax.ppermute(block, axis, [(i, (i + steps) % count) for i in range(count)]))
    return jnp.concatenate(arrived, axis=0)


def rms_scale(values, gain_vec):
    values = values.astype(jnp.float32)
    return values * lax.rsqrt(jnp.mean(values * values, axis=-1, keepdims=True) + EPS) * gain_vec


def rotary(values, positions):
    half_width = values.shape[-1] // 2
    frequency = 10000.0 ** (-jnp.arange(half_width, dtype=jnp.float32) / half_width)
    angles = positions.astype(jnp.float32)[:, None] * frequency[None, :]
    if values.ndim == 3:
        angles = angles[:, None, :]
    cosine = jnp.cos(angles)
    sine_part = jnp.sin(angles)
    lead_half = values[..., :half_width]
    tail_half = values[..., half_width:]
    return jnp.concatenate(
        [lead_half * cosine - tail_half * sine_part, lead_half * sine_part + tail_half * cosine],
        axis=-1,
    )


def positions_of(segment_row, segment_count):
    labels = jnp.arange(segment_count, dtype=jnp.int32)
    starts = jnp.sum((segment_row[None, :] < labels[:, None]).astype(jnp.int32), axis=1)
    member = (segment_row[:, None] == labels[None, :]).astype(jnp.int32)
    return jnp.arange(segment_row.shape[0], dtype=jnp.int32) - jnp.sum(
        member * starts[None, :], axis=1
    )


def shards(
    layer_input,
    segment_ids,
    route_ids,
    route_weights,
    attn_gain,
    w_query,
    w_kv_down,
    latent_gain,
    w_kv_up,
    w_out,
    ffn_gain,
    w_shared_gate,
    w_shared_up,
    w_shared_down,
    w_expert_gate,
    w_expert_up,
    w_expert_down,
):
    n_mdl = lax.axis_size("mdl")
    n_wide = lax.axis_size(("tok", "mdl"))
    section_id = lax.axis_index("section")
    tok_rank = lax.axis_index("tok")
    mdl_rank = lax.axis_index("mdl")
    micro_count, tok_dev, model_width = layer_input.shape
    row_dev = tok_dev // n_mdl
    top_count = route_ids.shape[2]
    local_heads = w_out.shape[0] // VDIM
    qk_width = NOPE + ROPE
    score_scale = 1.0 / math.sqrt(qk_width)
    expert_dev = w_expert_gate.shape[0]
    expert_total = expert_dev * n_wide
    capacity = max(2, 3 * row_dev * top_count // (2 * expert_total))
    slot_total = expert_total * capacity
    slot_ids = jnp.arange(slot_total, dtype=jnp.int32)
    expert_labels = jnp.arange(expert_total, dtype=jnp.int32)

    segment_row = lax.dynamic_index_in_dim(segment_ids, section_id, 0, keepdims=False)
    rows_in = lax.dynamic_index_in_dim(layer_input, section_id, 0, keepdims=False)
    expert_ids = lax.dynamic_index_in_dim(route_ids, section_id, 0, keepdims=False).reshape(-1)
    weight_rows = lax.dynamic_index_in_dim(route_weights, section_id, 0, keepdims=False)

    positions = positions_of(segment_row, SEGS)
    query_start = tok_rank * tok_dev
    query_pos = lax.dynamic_slice_in_dim(positions, query_start, tok_dev)
    query_seg = lax.dynamic_slice_in_dim(segment_row, query_start, tok_dev)
    query_index = query_start + jnp.arange(tok_dev, dtype=jnp.int32)

    normed = rms_scale(rows_in, attn_gain).astype(jnp.bfloat16)
    queries = jnp.dot(normed, w_query, preferred_element_type=jnp.float32).reshape(
        tok_dev, local_heads, qk_width
    )
    queries = jnp.concatenate(
        [queries[..., :NOPE], rotary(queries[..., NOPE:], query_pos)], axis=-1
    ).astype(jnp.bfloat16)
    compressed = jnp.dot(normed, w_kv_down, preferred_element_type=jnp.float32)
    latent = rms_scale(compressed[:, :LATENT], latent_gain).astype(jnp.bfloat16)
    key_rope = rotary(compressed[:, LATENT:], query_pos).astype(jnp.bfloat16)
    n_tok = lax.axis_size("tok")
    reach = LONGEST_SEGMENT // tok_dev
    kv_own = jnp.concatenate([latent, key_rope], axis=-1)
    kv_parts = [kv_own]
    for steps in range(1, min(reach, n_tok - 1) + 1):
        kv_parts.insert(0, passed_along(kv_own, "tok", steps))
    kv_rows = jnp.concatenate(kv_parts, axis=0)
    key_count = kv_rows.shape[0]
    key_start = query_start + tok_dev - key_count
    expanded = (
        jnp.dot(kv_rows[:, :LATENT], w_kv_up, preferred_element_type=jnp.float32)
        .astype(jnp.bfloat16)
        .reshape(key_count, local_heads, NOPE + VDIM)
    )
    rope_keys = kv_rows[:, LATENT:]
    scores = jnp.einsum(
        "qhd,khd->hqk", queries[..., :NOPE], expanded[..., :NOPE],
        preferred_element_type=jnp.float32,
    )
    scores = scores + jnp.einsum(
        "qhd,kd->hqk", queries[..., NOPE:], rope_keys, preferred_element_type=jnp.float32
    )
    scores = scores * score_scale
    key_index = key_start + jnp.arange(key_count, dtype=jnp.int32)
    padded_seg = jnp.concatenate([jnp.full((key_count,), -1, jnp.int32), segment_row])
    key_seg = lax.dynamic_slice_in_dim(padded_seg, key_start + key_count, key_count)
    allowed = (
        (key_seg[None, :] == query_seg[:, None])
        & (key_index[None, :] <= query_index[:, None])
        & (key_index[None, :] >= 0)
    )
    allowed = allowed[None, :, :]
    masked = jnp.where(allowed, scores, -1e30)
    row_max = jnp.max(masked, axis=-1, keepdims=True)
    weights = jnp.where(allowed, jnp.exp(scores - row_max), 0.0)
    totals = jnp.sum(weights, axis=-1, keepdims=True)
    weighted = jnp.einsum(
        "hqk,khd->hqd", weights.astype(jnp.bfloat16), expanded[..., NOPE:],
        preferred_element_type=jnp.float32,
    )
    attended = (
        (weighted / totals).astype(jnp.bfloat16).transpose(1, 0, 2).reshape(tok_dev, local_heads * VDIM)
    )
    head_parts = jnp.dot(attended, w_out, preferred_element_type=jnp.float32).astype(jnp.bfloat16)
    mixed_heads = summed_over(head_parts, "mdl")
    own_input = lax.dynamic_slice_in_dim(rows_in, mdl_rank * row_dev, row_dev)
    own_residual = (own_input.astype(jnp.float32) + mixed_heads).astype(jnp.bfloat16)
    normed_ffn = rms_scale(own_residual, ffn_gain).astype(jnp.bfloat16)
    normed_ffn_all = gathered_over(normed_ffn, "mdl")

    gate_proj = jnp.dot(normed_ffn_all, w_shared_gate, preferred_element_type=jnp.float32)
    up_proj = jnp.dot(normed_ffn_all, w_shared_up, preferred_element_type=jnp.float32)
    shared_act = (jax.nn.silu(gate_proj) * up_proj).astype(jnp.bfloat16)
    shared_out = summed_over(
        jnp.dot(shared_act, w_shared_down, preferred_element_type=jnp.float32).astype(jnp.bfloat16),
        "mdl",
        arrival_order=True,
    )

    onehot = (expert_ids[:, None] == expert_labels[None, :]).astype(jnp.int32)
    earlier = jnp.cumsum(onehot, axis=0) - onehot
    slot_index = jnp.sum(earlier * onehot, axis=1)
    target = expert_ids * capacity + slot_index
    hit = slot_ids[:, None] == target[None, :]
    pair_row = jnp.arange(row_dev * top_count, dtype=jnp.int32) // top_count
    slot_row = jnp.where(
        jnp.any(hit, axis=1), jnp.sum(jnp.where(hit, pair_row[None, :], 0), axis=1), row_dev
    )
    padded_rows = jnp.concatenate([normed_ffn, jnp.zeros((1, model_width), normed_ffn.dtype)])
    outgoing = padded_rows[slot_row].reshape(n_wide, expert_dev, capacity, model_width)
    buffer = lax.all_to_all(outgoing, ("tok", "mdl"), split_axis=0, concat_axis=0, tiled=True)
    e_gate = jnp.einsum("sjkd,jdf->sjkf", buffer, w_expert_gate, preferred_element_type=jnp.float32)
    e_up = jnp.einsum("sjkd,jdf->sjkf", buffer, w_expert_up, preferred_element_type=jnp.float32)
    expert_act = (jax.nn.silu(e_gate) * e_up).astype(jnp.bfloat16)
    produced = jnp.einsum(
        "sjkf,jfd->sjkd", expert_act, w_expert_down, preferred_element_type=jnp.float32
    ).astype(jnp.bfloat16)
    returned = lax.all_to_all(produced, ("tok", "mdl"), split_axis=0, concat_axis=0, tiled=True)
    picked = returned.reshape(slot_total, model_width)[target].reshape(row_dev, top_count, model_width)
    routed = jnp.sum(picked.astype(jnp.float32) * weight_rows[:, :, None], axis=1)
    finished = (own_residual.astype(jnp.float32) + shared_out + routed).astype(jnp.bfloat16)
    return finished[None]


def solution(mesh):
    in_specs = (
        P(None, "tok", None),
        P(),
        P(None, ("tok", "mdl"), None),
        P(None, ("tok", "mdl"), None),
        P(),
        P(None, "mdl"),
        P(),
        P(),
        P(None, "mdl"),
        P("mdl", None),
        P(),
        P(None, "mdl"),
        P(None, "mdl"),
        P("mdl", None),
        P(("tok", "mdl"), None, None),
        P(("tok", "mdl"), None, None),
        P(("tok", "mdl"), None, None),
    )
    out_specs = P("section", ("tok", "mdl"), None)
    return jax.shard_map(shards, mesh=mesh, in_specs=in_specs, out_specs=out_specs, check_vma=False)
```

```python
import math

import jax
import jax.numpy as jnp
from jax import lax
from jax.sharding import PartitionSpec as P

NOPE = 128
ROPE = 64
VDIM = 128
LATENT = 512
SEGS = 4
LONGEST_SEGMENT = 1024


EPS = 1e-06


def passed_along(value, axis, steps):
    count = lax.axis_size(axis)
    initial, last = (max(0, -steps), min(count, count - steps))
    return lax.ppermute(value, axis, [(source, source + steps) for source in range(initial, last)])


def summed_over(parts, axis, arrival_order=False):
    count = lax.axis_size(axis)
    rank = lax.axis_index(axis)
    pieces = parts.reshape((count, parts.shape[0] // count) + parts.shape[1:])

    def piece_for(steps):
        if arrival_order:
            return pieces[(count - steps) % count]
        return lax.dynamic_index_in_dim(pieces, (rank + steps) % count, 0, keepdims=False)

    total = piece_for(0).astype(jnp.float32)
    for steps in range(1, count):
        moved = lax.ppermute(piece_for(steps), axis, [(i, (i + steps) % count) for i in range(count)])
        total = total + moved.astype(jnp.float32)
    return total


def gathered_over(block, axis):
    count = lax.axis_size(axis)
    arrived = [block]
    for steps in range(1, count):
        arrived.append(lax.ppermute(block, axis, [(i, (i + steps) % count) for i in range(count)]))
    return jnp.concatenate(arrived, axis=0)


def rms_scale(values, gain_vec):
    values = values.astype(jnp.float32)
    return values * lax.rsqrt(jnp.mean(values * values, axis=-1, keepdims=True) + EPS) * gain_vec


def rotary(values, positions):
    half_width = values.shape[-1] // 2
    frequency = 10000.0 ** (-jnp.arange(half_width, dtype=jnp.float32) / half_width)
    angles = positions.astype(jnp.float32)[:, None] * frequency[None, :]
    if values.ndim == 3:
        angles = angles[:, None, :]
    cosine = jnp.cos(angles)
    sine_part = jnp.sin(angles)
    lead_half = values[..., :half_width]
    tail_half = values[..., half_width:]
    return jnp.concatenate(
        [lead_half * cosine - tail_half * sine_part, lead_half * sine_part + tail_half * cosine],
        axis=-1,
    )


def positions_of(segment_row, segment_count):
    labels = jnp.arange(segment_count, dtype=jnp.int32)
    starts = jnp.sum((segment_row[None, :] < labels[:, None]).astype(jnp.int32), axis=1)
    member = (segment_row[:, None] == labels[None, :]).astype(jnp.int32)
    return jnp.arange(segment_row.shape[0], dtype=jnp.int32) - jnp.sum(
        member * starts[None, :], axis=1
    )


def shards(
    layer_input,
    segment_ids,
    route_ids,
    route_weights,
    attn_gain,
    w_query,
    w_kv_down,
    latent_gain,
    w_kv_up,
    w_out,
    ffn_gain,
    w_shared_gate,
    w_shared_up,
    w_shared_down,
    w_expert_gate,
    w_expert_up,
    w_expert_down,
):
    n_mdl = lax.axis_size("mdl")
    n_wide = lax.axis_size(("tok", "mdl"))
    section_id = lax.axis_index("section")
    tok_rank = lax.axis_index("tok")
    mdl_rank = lax.axis_index("mdl")
    micro_count, tok_dev, model_width = layer_input.shape
    row_dev = tok_dev // n_mdl
    top_count = route_ids.shape[2]
    local_heads = w_out.shape[0] // VDIM
    qk_width = NOPE + ROPE
    score_scale = 1.0 / math.sqrt(qk_width)
    expert_dev = w_expert_gate.shape[0]
    expert_total = expert_dev * n_wide
    capacity = max(2, 3 * row_dev * top_count // (2 * expert_total))
    slot_total = expert_total * capacity
    slot_ids = jnp.arange(slot_total, dtype=jnp.int32)
    expert_labels = jnp.arange(expert_total, dtype=jnp.int32)

    segment_row = lax.dynamic_index_in_dim(segment_ids, section_id, 0, keepdims=False)
    rows_in = lax.dynamic_index_in_dim(layer_input, section_id, 0, keepdims=False)
    expert_ids = lax.dynamic_index_in_dim(route_ids, section_id, 0, keepdims=False).reshape(-1)
    weight_rows = lax.dynamic_index_in_dim(route_weights, section_id, 0, keepdims=False)

    positions = positions_of(segment_row, SEGS)
    query_start = tok_rank * tok_dev
    query_pos = lax.dynamic_slice_in_dim(positions, query_start, tok_dev)
    query_seg = lax.dynamic_slice_in_dim(segment_row, query_start, tok_dev)
    query_index = query_start + jnp.arange(tok_dev, dtype=jnp.int32)

    normed = rms_scale(rows_in, attn_gain).astype(jnp.bfloat16)
    queries_t = jnp.einsum(
        "dc,qd->cq", w_query, normed, preferred_element_type=jnp.float32
    ).reshape(local_heads, qk_width, tok_dev)
    half_rope = ROPE // 2
    frequency = 10000.0 ** (-jnp.arange(half_rope, dtype=jnp.float32) / half_rope)
    angles = frequency[:, None] * query_pos.astype(jnp.float32)[None, :]
    cosine = jnp.cos(angles)[None]
    sine_part = jnp.sin(angles)[None]
    lead_half = queries_t[:, NOPE : NOPE + half_rope]
    tail_half = queries_t[:, NOPE + half_rope :]
    queries_t = jnp.concatenate(
        [
            queries_t[:, :NOPE],
            lead_half * cosine - tail_half * sine_part,
            lead_half * sine_part + tail_half * cosine,
        ],
        axis=1,
    ).astype(jnp.bfloat16)
    compressed = jnp.dot(normed, w_kv_down, preferred_element_type=jnp.float32)
    latent = rms_scale(compressed[:, :LATENT], latent_gain).astype(jnp.bfloat16)
    key_rope = rotary(compressed[:, LATENT:], query_pos).astype(jnp.bfloat16)
    n_tok = lax.axis_size("tok")
    reach = LONGEST_SEGMENT // tok_dev
    kv_own = jnp.concatenate([latent, key_rope], axis=-1)
    kv_parts = [kv_own]
    for steps in range(1, min(reach, n_tok - 1) + 1):
        kv_parts.insert(0, passed_along(kv_own, "tok", steps))
    kv_rows = jnp.concatenate(kv_parts, axis=0)
    key_count = kv_rows.shape[0]
    key_start = query_start + tok_dev - key_count
    expanded = (
        jnp.dot(kv_rows[:, :LATENT], w_kv_up, preferred_element_type=jnp.float32)
        .astype(jnp.bfloat16)
        .reshape(key_count, local_heads, NOPE + VDIM)
    )
    rope_keys = kv_rows[:, LATENT:]
    scores = jnp.einsum(
        "hdq,khd->hqk", queries_t[:, :NOPE], expanded[..., :NOPE],
        preferred_element_type=jnp.float32,
    )
    scores = scores + jnp.einsum(
        "hdq,kd->hqk", queries_t[:, NOPE:], rope_keys, preferred_element_type=jnp.float32
    )
    scores = scores * score_scale
    key_index = key_start + jnp.arange(key_count, dtype=jnp.int32)
    padded_seg = jnp.concatenate([jnp.full((key_count,), -1, jnp.int32), segment_row])
    key_seg = lax.dynamic_slice_in_dim(padded_seg, key_start + key_count, key_count)
    allowed = (
        (key_seg[None, :] == query_seg[:, None])
        & (key_index[None, :] <= query_index[:, None])
        & (key_index[None, :] >= 0)
    )
    allowed = allowed[None, :, :]
    masked = jnp.where(allowed, scores, -1e30)
    row_max = jnp.max(masked, axis=-1, keepdims=True)
    weights = jnp.where(allowed, jnp.exp(scores - row_max), 0.0)
    totals = jnp.sum(weights, axis=-1, keepdims=True)
    weighted = jnp.einsum(
        "hqk,khd->hqd", weights.astype(jnp.bfloat16), expanded[..., NOPE:],
        preferred_element_type=jnp.float32,
    )
    attended = (
        (weighted / totals).astype(jnp.bfloat16).transpose(1, 0, 2).reshape(tok_dev, local_heads * VDIM)
    )
    head_parts = jnp.dot(attended, w_out, preferred_element_type=jnp.float32).astype(jnp.bfloat16)
    mixed_heads = summed_over(head_parts, "mdl")
    own_input = lax.dynamic_slice_in_dim(rows_in, mdl_rank * row_dev, row_dev)
    own_residual = (own_input.astype(jnp.float32) + mixed_heads).astype(jnp.bfloat16)
    normed_ffn = rms_scale(own_residual, ffn_gain).astype(jnp.bfloat16)
    normed_ffn_all = gathered_over(normed_ffn, "mdl")

    gate_proj = jnp.dot(normed_ffn_all, w_shared_gate, preferred_element_type=jnp.float32)
    up_proj = jnp.dot(normed_ffn_all, w_shared_up, preferred_element_type=jnp.float32)
    shared_act = (jax.nn.silu(gate_proj) * up_proj).astype(jnp.bfloat16)
    shared_out = summed_over(
        jnp.dot(shared_act, w_shared_down, preferred_element_type=jnp.float32).astype(jnp.bfloat16),
        "mdl",
        arrival_order=True,
    )

    onehot = (expert_ids[:, None] == expert_labels[None, :]).astype(jnp.int32)
    earlier = jnp.cumsum(onehot, axis=0) - onehot
    slot_index = jnp.sum(earlier * onehot, axis=1)
    target = expert_ids * capacity + slot_index
    placing = (
        (slot_ids[:, None] == target[None, :])
        .astype(jnp.int32)
        .reshape(slot_total, row_dev, top_count)
    )
    placing = (
        jnp.sum(placing, axis=2)
        .astype(jnp.bfloat16)
        .reshape(n_wide, expert_dev, capacity, row_dev)
    )
    outgoing = jnp.einsum(
        "sjkr,rd->sjkd", placing, normed_ffn, preferred_element_type=jnp.float32
    ).astype(jnp.bfloat16)
    buffer = lax.all_to_all(outgoing, ("tok", "mdl"), split_axis=0, concat_axis=0, tiled=True)
    e_gate = jnp.einsum("sjkd,jdf->sjkf", buffer, w_expert_gate, preferred_element_type=jnp.float32)
    e_up = jnp.einsum("sjkd,jdf->sjkf", buffer, w_expert_up, preferred_element_type=jnp.float32)
    expert_act = (jax.nn.silu(e_gate) * e_up).astype(jnp.bfloat16)
    produced = jnp.einsum(
        "sjkf,jfd->sjkd", expert_act, w_expert_down, preferred_element_type=jnp.float32
    ).astype(jnp.bfloat16)
    returned = lax.all_to_all(produced, ("tok", "mdl"), split_axis=0, concat_axis=0, tiled=True)
    matched = target.reshape(row_dev, top_count)[:, :, None] == slot_ids[None, None, :]
    combining = jnp.sum(jnp.where(matched, weight_rows[:, :, None], 0.0), axis=1).reshape(
        row_dev, n_wide, expert_dev, capacity
    )
    routed = jnp.einsum(
        "rsjk,sjkd->rd",
        combining,
        returned.astype(jnp.float32),
        precision=lax.Precision.HIGHEST,
    )
    finished = (own_residual.astype(jnp.float32) + shared_out + routed).astype(jnp.bfloat16)
    return finished[None]


def solution(mesh):
    in_specs = (
        P(None, "tok", None),
        P(),
        P(None, ("tok", "mdl"), None),
        P(None, ("tok", "mdl"), None),
        P(),
        P(None, "mdl"),
        P(),
        P(),
        P(None, "mdl"),
        P("mdl", None),
        P(),
        P(None, "mdl"),
        P(None, "mdl"),
        P("mdl", None),
        P(("tok", "mdl"), None, None),
        P(("tok", "mdl"), None, None),
        P(("tok", "mdl"), None, None),
    )
    out_specs = P("section", ("tok", "mdl"), None)
    return jax.shard_map(shards, mesh=mesh, in_specs=in_specs, out_specs=out_specs, check_vma=False)
```

```python
import math

import jax
import jax.numpy as jnp
from jax import lax
from jax.sharding import PartitionSpec as P

NOPE = 128
ROPE = 64
VDIM = 128
LATENT = 512
SEGS = 4
LONGEST_SEGMENT = 1024


EPS = 1e-06


def passed_along(value, axis, steps):
    count = lax.axis_size(axis)
    initial, last = (max(0, -steps), min(count, count - steps))
    return lax.ppermute(value, axis, [(source, source + steps) for source in range(initial, last)])


def summed_over(parts, axis, arrival_order=False):
    count = lax.axis_size(axis)
    rank = lax.axis_index(axis)
    pieces = parts.reshape((count, parts.shape[0] // count) + parts.shape[1:])

    def piece_for(steps):
        if arrival_order:
            return pieces[(count - steps) % count]
        return lax.dynamic_index_in_dim(pieces, (rank + steps) % count, 0, keepdims=False)

    total = piece_for(0).astype(jnp.float32)
    for steps in range(1, count):
        moved = lax.ppermute(piece_for(steps), axis, [(i, (i + steps) % count) for i in range(count)])
        total = total + moved.astype(jnp.float32)
    return total


def gathered_over(block, axis):
    count = lax.axis_size(axis)
    arrived = [block]
    for steps in range(1, count):
        arrived.append(lax.ppermute(block, axis, [(i, (i + steps) % count) for i in range(count)]))
    return jnp.concatenate(arrived, axis=0)


def rms_scale(values, gain_vec):
    values = values.astype(jnp.float32)
    return values * lax.rsqrt(jnp.mean(values * values, axis=-1, keepdims=True) + EPS) * gain_vec


def rotary(values, positions):
    half_width = values.shape[-1] // 2
    frequency = 10000.0 ** (-jnp.arange(half_width, dtype=jnp.float32) / half_width)
    angles = positions.astype(jnp.float32)[:, None] * frequency[None, :]
    if values.ndim == 3:
        angles = angles[:, None, :]
    cosine = jnp.cos(angles)
    sine_part = jnp.sin(angles)
    lead_half = values[..., :half_width]
    tail_half = values[..., half_width:]
    return jnp.concatenate(
        [lead_half * cosine - tail_half * sine_part, lead_half * sine_part + tail_half * cosine],
        axis=-1,
    )


def positions_of(segment_row, segment_count):
    labels = jnp.arange(segment_count, dtype=jnp.int32)
    starts = jnp.sum((segment_row[None, :] < labels[:, None]).astype(jnp.int32), axis=1)
    member = (segment_row[:, None] == labels[None, :]).astype(jnp.int32)
    return jnp.arange(segment_row.shape[0], dtype=jnp.int32) - jnp.sum(
        member * starts[None, :], axis=1
    )


def shards(
    layer_input,
    segment_ids,
    route_ids,
    route_weights,
    attn_gain,
    w_query,
    w_kv_down,
    latent_gain,
    w_kv_up,
    w_out,
    ffn_gain,
    w_shared_gate,
    w_shared_up,
    w_shared_down,
    w_expert_gate,
    w_expert_up,
    w_expert_down,
):
    n_mdl = lax.axis_size("mdl")
    n_wide = lax.axis_size(("tok", "mdl"))
    section_id = lax.axis_index("section")
    tok_rank = lax.axis_index("tok")
    mdl_rank = lax.axis_index("mdl")
    micro_count, tok_dev, model_width = layer_input.shape
    row_dev = tok_dev // n_mdl
    top_count = route_ids.shape[2]
    local_heads = w_out.shape[0] // VDIM
    qk_width = NOPE + ROPE
    score_scale = 1.0 / math.sqrt(qk_width)
    expert_dev = w_expert_gate.shape[0]
    expert_total = expert_dev * n_wide
    capacity = max(2, 3 * row_dev * top_count // (2 * expert_total))
    slot_total = expert_total * capacity
    slot_ids = jnp.arange(slot_total, dtype=jnp.int32)
    expert_labels = jnp.arange(expert_total, dtype=jnp.int32)

    segment_row = lax.dynamic_index_in_dim(segment_ids, section_id, 0, keepdims=False)
    rows_in = lax.dynamic_index_in_dim(layer_input, section_id, 0, keepdims=False)
    expert_ids = lax.dynamic_index_in_dim(route_ids, section_id, 0, keepdims=False).reshape(-1)
    weight_rows = lax.dynamic_index_in_dim(route_weights, section_id, 0, keepdims=False)

    positions = positions_of(segment_row, SEGS)
    query_start = tok_rank * tok_dev
    query_pos = lax.dynamic_slice_in_dim(positions, query_start, tok_dev)
    query_seg = lax.dynamic_slice_in_dim(segment_row, query_start, tok_dev)
    query_index = query_start + jnp.arange(tok_dev, dtype=jnp.int32)

    normed = rms_scale(rows_in, attn_gain).astype(jnp.bfloat16)
    queries = jnp.dot(normed, w_query, preferred_element_type=jnp.float32).reshape(
        tok_dev, local_heads, qk_width
    )
    queries = jnp.concatenate(
        [queries[..., :NOPE], rotary(queries[..., NOPE:], query_pos)], axis=-1
    ).astype(jnp.bfloat16)
    compressed = jnp.dot(normed, w_kv_down, preferred_element_type=jnp.float32)
    latent = rms_scale(compressed[:, :LATENT], latent_gain).astype(jnp.bfloat16)
    key_rope = rotary(compressed[:, LATENT:], query_pos).astype(jnp.bfloat16)
    n_tok = lax.axis_size("tok")
    reach = LONGEST_SEGMENT // tok_dev
    kv_own = jnp.concatenate([latent, key_rope], axis=-1)
    kv_parts = [kv_own]
    for steps in range(1, min(reach, n_tok - 1) + 1):
        kv_parts.insert(0, passed_along(kv_own, "tok", steps))
    kv_rows = jnp.concatenate(kv_parts, axis=0)
    key_count = kv_rows.shape[0]
    key_start = query_start + tok_dev - key_count
    expanded = (
        jnp.dot(kv_rows[:, :LATENT], w_kv_up, preferred_element_type=jnp.float32)
        .astype(jnp.bfloat16)
        .reshape(key_count, local_heads, NOPE + VDIM)
    )
    rope_keys = kv_rows[:, LATENT:]
    scores = jnp.einsum(
        "qhd,khd->hqk", queries[..., :NOPE], expanded[..., :NOPE],
        preferred_element_type=jnp.float32,
    )
    scores = scores + jnp.einsum(
        "qhd,kd->hqk", queries[..., NOPE:], rope_keys, preferred_element_type=jnp.float32
    )
    scores = scores * score_scale
    key_index = key_start + jnp.arange(key_count, dtype=jnp.int32)
    padded_seg = jnp.concatenate([jnp.full((key_count,), -1, jnp.int32), segment_row])
    key_seg = lax.dynamic_slice_in_dim(padded_seg, key_start + key_count, key_count)
    allowed = (
        (key_seg[None, :] == query_seg[:, None])
        & (key_index[None, :] <= query_index[:, None])
        & (key_index[None, :] >= 0)
    )
    allowed = allowed[None, :, :]
    masked = jnp.where(allowed, scores, -1e30)
    row_max = jnp.max(masked, axis=-1, keepdims=True)
    weights = jnp.where(allowed, jnp.exp(scores - row_max), 0.0)
    totals = jnp.sum(weights, axis=-1, keepdims=True)
    weighted = jnp.einsum(
        "hqk,khd->hqd", weights.astype(jnp.bfloat16), expanded[..., NOPE:],
        preferred_element_type=jnp.float32,
    )
    attended = (
        (weighted / totals).astype(jnp.bfloat16).transpose(1, 0, 2).reshape(tok_dev, local_heads * VDIM)
    )
    head_parts = jnp.dot(attended, w_out, preferred_element_type=jnp.float32).astype(jnp.bfloat16)
    mixed_heads = summed_over(head_parts, "mdl")
    own_input = lax.dynamic_slice_in_dim(rows_in, mdl_rank * row_dev, row_dev)
    own_residual = (own_input.astype(jnp.float32) + mixed_heads).astype(jnp.bfloat16)
    normed_ffn = rms_scale(own_residual, ffn_gain).astype(jnp.bfloat16)
    normed_ffn_all = gathered_over(normed_ffn, "mdl")

    gate_proj = jnp.dot(normed_ffn_all, w_shared_gate, preferred_element_type=jnp.float32)
    up_proj = jnp.dot(normed_ffn_all, w_shared_up, preferred_element_type=jnp.float32)
    shared_act = (jax.nn.silu(gate_proj) * up_proj).astype(jnp.bfloat16)
    shared_out = summed_over(
        jnp.dot(shared_act, w_shared_down, preferred_element_type=jnp.float32).astype(jnp.bfloat16),
        "mdl",
        arrival_order=True,
    )

    onehot = (expert_ids[:, None] == expert_labels[None, :]).astype(jnp.int32)
    earlier = jnp.cumsum(onehot, axis=0) - onehot
    slot_index = jnp.sum(earlier * onehot, axis=1)
    target = expert_ids * capacity + slot_index
    placing = (
        (slot_ids[:, None] == target[None, :])
        .astype(jnp.int32)
        .reshape(slot_total, row_dev, top_count)
    )
    placing = (
        jnp.sum(placing, axis=2)
        .astype(jnp.bfloat16)
        .reshape(n_wide, expert_dev, capacity, row_dev)
    )
    outgoing = jnp.einsum(
        "sjkr,rd->sjkd", placing, normed_ffn, preferred_element_type=jnp.float32
    ).astype(jnp.bfloat16)
    buffer = lax.all_to_all(outgoing, ("tok", "mdl"), split_axis=0, concat_axis=0, tiled=True)
    e_gate = jnp.einsum("sjkd,jdf->sjkf", buffer, w_expert_gate, preferred_element_type=jnp.float32)
    e_up = jnp.einsum("sjkd,jdf->sjkf", buffer, w_expert_up, preferred_element_type=jnp.float32)
    expert_act = (jax.nn.silu(e_gate) * e_up).astype(jnp.bfloat16)
    produced = jnp.einsum(
        "sjkf,jfd->sjkd", expert_act, w_expert_down, preferred_element_type=jnp.float32
    ).astype(jnp.bfloat16)
    returned = lax.all_to_all(produced, ("tok", "mdl"), split_axis=0, concat_axis=0, tiled=True)
    matched = target.reshape(row_dev, top_count)[:, :, None] == slot_ids[None, None, :]
    combining = jnp.sum(jnp.where(matched, weight_rows[:, :, None], 0.0), axis=1).reshape(
        row_dev, n_wide, expert_dev, capacity
    )
    routed = jnp.einsum(
        "rsjk,sjkd->rd",
        combining,
        returned.astype(jnp.float32),
        precision=lax.Precision.HIGH,
    )
    finished = (own_residual.astype(jnp.float32) + shared_out + routed).astype(jnp.bfloat16)
    return finished[None]


def solution(mesh):
    in_specs = (
        P(None, "tok", None),
        P(),
        P(None, ("tok", "mdl"), None),
        P(None, ("tok", "mdl"), None),
        P(),
        P(None, "mdl"),
        P(),
        P(),
        P(None, "mdl"),
        P("mdl", None),
        P(),
        P(None, "mdl"),
        P(None, "mdl"),
        P("mdl", None),
        P(("tok", "mdl"), None, None),
        P(("tok", "mdl"), None, None),
        P(("tok", "mdl"), None, None),
    )
    out_specs = P("section", ("tok", "mdl"), None)
    return jax.shard_map(shards, mesh=mesh, in_specs=in_specs, out_specs=out_specs, check_vma=False)
```

```python
import math

import jax
import jax.numpy as jnp
from jax import lax
from jax.sharding import PartitionSpec as P

NOPE = 128
ROPE = 64
VDIM = 128
LATENT = 512
SEGS = 4
LONGEST_SEGMENT = 1024


EPS = 1e-06


def passed_along(value, axis, steps):
    count = lax.axis_size(axis)
    initial, last = (max(0, -steps), min(count, count - steps))
    return lax.ppermute(value, axis, [(source, source + steps) for source in range(initial, last)])


def summed_over(parts, axis, arrival_order=False):
    count = lax.axis_size(axis)
    rank = lax.axis_index(axis)
    pieces = parts.reshape((count, parts.shape[0] // count) + parts.shape[1:])

    def piece_for(steps):
        if arrival_order:
            return pieces[(count - steps) % count]
        return lax.dynamic_index_in_dim(pieces, (rank + steps) % count, 0, keepdims=False)

    total = piece_for(0).astype(jnp.float32)
    for steps in range(1, count):
        moved = lax.ppermute(piece_for(steps), axis, [(i, (i + steps) % count) for i in range(count)])
        total = total + moved.astype(jnp.float32)
    return total


def gathered_over(block, axis):
    count = lax.axis_size(axis)
    arrived = [block]
    for steps in range(1, count):
        arrived.append(lax.ppermute(block, axis, [(i, (i + steps) % count) for i in range(count)]))
    return jnp.concatenate(arrived, axis=0)


def rms_scale(values, gain_vec):
    values = values.astype(jnp.float32)
    return values * lax.rsqrt(jnp.mean(values * values, axis=-1, keepdims=True) + EPS) * gain_vec


def rotary(values, positions):
    half_width = values.shape[-1] // 2
    frequency = 10000.0 ** (-jnp.arange(half_width, dtype=jnp.float32) / half_width)
    angles = positions.astype(jnp.float32)[:, None] * frequency[None, :]
    if values.ndim == 3:
        angles = angles[:, None, :]
    cosine = jnp.cos(angles)
    sine_part = jnp.sin(angles)
    lead_half = values[..., :half_width]
    tail_half = values[..., half_width:]
    return jnp.concatenate(
        [lead_half * cosine - tail_half * sine_part, lead_half * sine_part + tail_half * cosine],
        axis=-1,
    )


def positions_of(segment_row, segment_count):
    labels = jnp.arange(segment_count, dtype=jnp.int32)
    starts = jnp.sum((segment_row[None, :] < labels[:, None]).astype(jnp.int32), axis=1)
    member = (segment_row[:, None] == labels[None, :]).astype(jnp.int32)
    return jnp.arange(segment_row.shape[0], dtype=jnp.int32) - jnp.sum(
        member * starts[None, :], axis=1
    )


def shards(
    layer_input,
    segment_ids,
    route_ids,
    route_weights,
    attn_gain,
    w_query,
    w_kv_down,
    latent_gain,
    w_kv_up,
    w_out,
    ffn_gain,
    w_shared_gate,
    w_shared_up,
    w_shared_down,
    w_expert_gate,
    w_expert_up,
    w_expert_down,
):
    n_mdl = lax.axis_size("mdl")
    n_wide = lax.axis_size(("tok", "mdl"))
    section_id = lax.axis_index("section")
    tok_rank = lax.axis_index("tok")
    mdl_rank = lax.axis_index("mdl")
    micro_count, tok_dev, model_width = layer_input.shape
    row_dev = tok_dev // n_mdl
    top_count = route_ids.shape[2]
    local_heads = w_out.shape[0] // VDIM
    qk_width = NOPE + ROPE
    score_scale = 1.0 / math.sqrt(qk_width)
    expert_dev = w_expert_gate.shape[0]
    expert_total = expert_dev * n_wide
    capacity = max(2, 3 * row_dev * top_count // (2 * expert_total))
    slot_total = expert_total * capacity
    slot_ids = jnp.arange(slot_total, dtype=jnp.int32)
    expert_labels = jnp.arange(expert_total, dtype=jnp.int32)

    segment_row = lax.dynamic_index_in_dim(segment_ids, section_id, 0, keepdims=False)
    rows_in = lax.dynamic_index_in_dim(layer_input, section_id, 0, keepdims=False)
    expert_ids = lax.dynamic_index_in_dim(route_ids, section_id, 0, keepdims=False).reshape(-1)
    weight_rows = lax.dynamic_index_in_dim(route_weights, section_id, 0, keepdims=False)

    positions = positions_of(segment_row, SEGS)
    query_start = tok_rank * tok_dev
    query_pos = lax.dynamic_slice_in_dim(positions, query_start, tok_dev)
    query_seg = lax.dynamic_slice_in_dim(segment_row, query_start, tok_dev)
    query_index = query_start + jnp.arange(tok_dev, dtype=jnp.int32)

    normed = rms_scale(rows_in, attn_gain).astype(jnp.bfloat16)
    queries_t = jnp.einsum(
        "dc,qd->cq", w_query, normed, preferred_element_type=jnp.float32
    ).reshape(local_heads, qk_width, tok_dev)
    half_rope = ROPE // 2
    frequency = 10000.0 ** (-jnp.arange(half_rope, dtype=jnp.float32) / half_rope)
    angles = frequency[:, None] * query_pos.astype(jnp.float32)[None, :]
    cosine = jnp.cos(angles)[None]
    sine_part = jnp.sin(angles)[None]
    lead_half = queries_t[:, NOPE : NOPE + half_rope]
    tail_half = queries_t[:, NOPE + half_rope :]
    queries_t = jnp.concatenate(
        [
            queries_t[:, :NOPE],
            lead_half * cosine - tail_half * sine_part,
            lead_half * sine_part + tail_half * cosine,
        ],
        axis=1,
    ).astype(jnp.bfloat16)
    compressed = jnp.dot(normed, w_kv_down, preferred_element_type=jnp.float32)
    latent = rms_scale(compressed[:, :LATENT], latent_gain).astype(jnp.bfloat16)
    key_rope = rotary(compressed[:, LATENT:], query_pos).astype(jnp.bfloat16)
    n_tok = lax.axis_size("tok")
    reach = LONGEST_SEGMENT // tok_dev
    kv_own = jnp.concatenate([latent, key_rope], axis=-1)
    kv_parts = [kv_own]
    for steps in range(1, min(reach, n_tok - 1) + 1):
        kv_parts.insert(0, passed_along(kv_own, "tok", steps))
    kv_rows = jnp.concatenate(kv_parts, axis=0)
    key_count = kv_rows.shape[0]
    key_start = query_start + tok_dev - key_count
    expanded = (
        jnp.dot(kv_rows[:, :LATENT], w_kv_up, preferred_element_type=jnp.float32)
        .astype(jnp.bfloat16)
        .reshape(key_count, local_heads, NOPE + VDIM)
    )
    rope_keys = kv_rows[:, LATENT:]
    scores = jnp.einsum(
        "hdq,khd->hqk", queries_t[:, :NOPE], expanded[..., :NOPE],
        preferred_element_type=jnp.float32,
    )
    scores = scores + jnp.einsum(
        "hdq,kd->hqk", queries_t[:, NOPE:], rope_keys, preferred_element_type=jnp.float32
    )
    scores = scores * score_scale
    key_index = key_start + jnp.arange(key_count, dtype=jnp.int32)
    padded_seg = jnp.concatenate([jnp.full((key_count,), -1, jnp.int32), segment_row])
    key_seg = lax.dynamic_slice_in_dim(padded_seg, key_start + key_count, key_count)
    allowed = (
        (key_seg[None, :] == query_seg[:, None])
        & (key_index[None, :] <= query_index[:, None])
        & (key_index[None, :] >= 0)
    )
    allowed = allowed[None, :, :]
    masked = jnp.where(allowed, scores, -1e30)
    row_max = jnp.max(masked, axis=-1, keepdims=True)
    weights = jnp.where(allowed, jnp.exp(scores - row_max), 0.0)
    totals = jnp.sum(weights, axis=-1, keepdims=True)
    weighted = jnp.einsum(
        "hqk,khd->hqd", weights.astype(jnp.bfloat16), expanded[..., NOPE:],
        preferred_element_type=jnp.float32,
    )
    attended = (
        (weighted / totals).astype(jnp.bfloat16).transpose(1, 0, 2).reshape(tok_dev, local_heads * VDIM)
    )
    head_parts = jnp.dot(attended, w_out, preferred_element_type=jnp.float32).astype(jnp.bfloat16)
    mixed_heads = summed_over(head_parts, "mdl")
    own_input = lax.dynamic_slice_in_dim(rows_in, mdl_rank * row_dev, row_dev)
    own_residual = (own_input.astype(jnp.float32) + mixed_heads).astype(jnp.bfloat16)
    normed_ffn = rms_scale(own_residual, ffn_gain).astype(jnp.bfloat16)
    normed_ffn_all = gathered_over(normed_ffn, "mdl")

    gate_proj = jnp.dot(normed_ffn_all, w_shared_gate, preferred_element_type=jnp.float32)
    up_proj = jnp.dot(normed_ffn_all, w_shared_up, preferred_element_type=jnp.float32)
    shared_act = (jax.nn.silu(gate_proj) * up_proj).astype(jnp.bfloat16)
    shared_out = summed_over(
        jnp.dot(shared_act, w_shared_down, preferred_element_type=jnp.float32).astype(jnp.bfloat16),
        "mdl",
        arrival_order=True,
    )

    onehot = (expert_ids[:, None] == expert_labels[None, :]).astype(jnp.int32)
    earlier = jnp.cumsum(onehot, axis=0) - onehot
    slot_index = jnp.sum(earlier * onehot, axis=1)
    target = expert_ids * capacity + slot_index
    placing = (
        (slot_ids[:, None] == target[None, :])
        .astype(jnp.int32)
        .reshape(slot_total, row_dev, top_count)
    )
    placing = (
        jnp.sum(placing, axis=2)
        .astype(jnp.bfloat16)
        .reshape(n_wide, expert_dev, capacity, row_dev)
    )
    outgoing = jnp.einsum(
        "sjkr,rd->sjkd", placing, normed_ffn, preferred_element_type=jnp.float32
    ).astype(jnp.bfloat16)
    buffer = lax.all_to_all(outgoing, ("tok", "mdl"), split_axis=0, concat_axis=0, tiled=True)
    e_gate = jnp.einsum("sjkd,jdf->sjkf", buffer, w_expert_gate, preferred_element_type=jnp.float32)
    e_up = jnp.einsum("sjkd,jdf->sjkf", buffer, w_expert_up, preferred_element_type=jnp.float32)
    expert_act = (jax.nn.silu(e_gate) * e_up).astype(jnp.bfloat16)
    produced = jnp.einsum(
        "sjkf,jfd->sjkd", expert_act, w_expert_down, preferred_element_type=jnp.float32
    ).astype(jnp.bfloat16)
    returned = lax.all_to_all(produced, ("tok", "mdl"), split_axis=0, concat_axis=0, tiled=True)
    matched = target.reshape(row_dev, top_count)[:, :, None] == slot_ids[None, None, :]
    combining = jnp.sum(jnp.where(matched, weight_rows[:, :, None], 0.0), axis=1).reshape(
        row_dev, n_wide, expert_dev, capacity
    )
    routed = jnp.einsum(
        "rsjk,sjkd->rd",
        combining,
        returned.astype(jnp.float32),
        precision=lax.Precision.HIGH,
    )
    finished = (own_residual.astype(jnp.float32) + shared_out + routed).astype(jnp.bfloat16)
    return finished[None]


def solution(mesh):
    in_specs = (
        P(None, "tok", None),
        P(),
        P(None, ("tok", "mdl"), None),
        P(None, ("tok", "mdl"), None),
        P(),
        P(None, "mdl"),
        P(),
        P(),
        P(None, "mdl"),
        P("mdl", None),
        P(),
        P(None, "mdl"),
        P(None, "mdl"),
        P("mdl", None),
        P(("tok", "mdl"), None, None),
        P(("tok", "mdl"), None, None),
        P(("tok", "mdl"), None, None),
    )
    out_specs = P("section", ("tok", "mdl"), None)
    return jax.shard_map(shards, mesh=mesh, in_specs=in_specs, out_specs=out_specs, check_vma=False)
```

```python
import math

import jax
import jax.numpy as jnp
from jax import lax
from jax.sharding import PartitionSpec as P

NOPE = 128
ROPE = 64
VDIM = 128
LATENT = 512
SEGS = 4
LONGEST_SEGMENT = 1024


EPS = 1e-06


def passed_along(value, axis, steps):
    count = lax.axis_size(axis)
    initial, last = (max(0, -steps), min(count, count - steps))
    return lax.ppermute(value, axis, [(source, source + steps) for source in range(initial, last)])


def summed_over(parts, axis, arrival_order=False):
    count = lax.axis_size(axis)
    rank = lax.axis_index(axis)
    pieces = parts.reshape((count, parts.shape[0] // count) + parts.shape[1:])

    def piece_for(steps):
        if arrival_order:
            return pieces[(count - steps) % count]
        return lax.dynamic_index_in_dim(pieces, (rank + steps) % count, 0, keepdims=False)

    total = piece_for(0).astype(jnp.float32)
    for steps in range(1, count):
        moved = lax.ppermute(piece_for(steps), axis, [(i, (i + steps) % count) for i in range(count)])
        total = total + moved.astype(jnp.float32)
    return total


def gathered_over(block, axis):
    count = lax.axis_size(axis)
    arrived = [block]
    for steps in range(1, count):
        arrived.append(lax.ppermute(block, axis, [(i, (i + steps) % count) for i in range(count)]))
    return jnp.concatenate(arrived, axis=0)


def rms_scale(values, gain_vec):
    values = values.astype(jnp.float32)
    return values * lax.rsqrt(jnp.mean(values * values, axis=-1, keepdims=True) + EPS) * gain_vec


def rotary(values, positions):
    half_width = values.shape[-1] // 2
    frequency = 10000.0 ** (-jnp.arange(half_width, dtype=jnp.float32) / half_width)
    angles = positions.astype(jnp.float32)[:, None] * frequency[None, :]
    if values.ndim == 3:
        angles = angles[:, None, :]
    cosine = jnp.cos(angles)
    sine_part = jnp.sin(angles)
    lead_half = values[..., :half_width]
    tail_half = values[..., half_width:]
    return jnp.concatenate(
        [lead_half * cosine - tail_half * sine_part, lead_half * sine_part + tail_half * cosine],
        axis=-1,
    )


def positions_of(segment_row, segment_count):
    labels = jnp.arange(segment_count, dtype=jnp.int32)
    starts = jnp.sum((segment_row[None, :] < labels[:, None]).astype(jnp.int32), axis=1)
    member = (segment_row[:, None] == labels[None, :]).astype(jnp.int32)
    return jnp.arange(segment_row.shape[0], dtype=jnp.int32) - jnp.sum(
        member * starts[None, :], axis=1
    )


def shards(
    layer_input,
    segment_ids,
    route_ids,
    route_weights,
    attn_gain,
    w_query,
    w_kv_down,
    latent_gain,
    w_kv_up,
    w_out,
    ffn_gain,
    w_shared_gate,
    w_shared_up,
    w_shared_down,
    w_expert_gate,
    w_expert_up,
    w_expert_down,
):
    n_mdl = lax.axis_size("mdl")
    n_wide = lax.axis_size(("tok", "mdl"))
    section_id = lax.axis_index("section")
    tok_rank = lax.axis_index("tok")
    mdl_rank = lax.axis_index("mdl")
    micro_count, tok_dev, model_width = layer_input.shape
    row_dev = tok_dev // n_mdl
    top_count = route_ids.shape[2]
    local_heads = w_out.shape[0] // VDIM
    qk_width = NOPE + ROPE
    score_scale = 1.0 / math.sqrt(qk_width)
    expert_dev = w_expert_gate.shape[0]
    expert_total = expert_dev * n_wide
    capacity = max(2, 3 * row_dev * top_count // (2 * expert_total))
    slot_total = expert_total * capacity
    slot_ids = jnp.arange(slot_total, dtype=jnp.int32)
    expert_labels = jnp.arange(expert_total, dtype=jnp.int32)

    segment_row = lax.dynamic_index_in_dim(segment_ids, section_id, 0, keepdims=False)
    rows_in = lax.dynamic_index_in_dim(layer_input, section_id, 0, keepdims=False)
    expert_ids = lax.dynamic_index_in_dim(route_ids, section_id, 0, keepdims=False).reshape(-1)
    weight_rows = lax.dynamic_index_in_dim(route_weights, section_id, 0, keepdims=False)

    positions = positions_of(segment_row, SEGS)
    query_start = tok_rank * tok_dev
    query_pos = lax.dynamic_slice_in_dim(positions, query_start, tok_dev)
    query_seg = lax.dynamic_slice_in_dim(segment_row, query_start, tok_dev)
    query_index = query_start + jnp.arange(tok_dev, dtype=jnp.int32)

    normed = rms_scale(rows_in, attn_gain).astype(jnp.bfloat16)
    queries_t = jnp.einsum(
        "dc,qd->cq", w_query, normed, preferred_element_type=jnp.float32
    ).reshape(local_heads, qk_width, tok_dev)
    half_rope = ROPE // 2
    frequency = 10000.0 ** (-jnp.arange(half_rope, dtype=jnp.float32) / half_rope)
    angles = frequency[:, None] * query_pos.astype(jnp.float32)[None, :]
    cosine = jnp.cos(angles)[None]
    sine_part = jnp.sin(angles)[None]
    lead_half = queries_t[:, NOPE : NOPE + half_rope]
    tail_half = queries_t[:, NOPE + half_rope :]
    queries_t = jnp.concatenate(
        [
            queries_t[:, :NOPE],
            lead_half * cosine - tail_half * sine_part,
            lead_half * sine_part + tail_half * cosine,
        ],
        axis=1,
    ).astype(jnp.bfloat16)
    compressed = jnp.dot(normed, w_kv_down, preferred_element_type=jnp.float32)
    latent = rms_scale(compressed[:, :LATENT], latent_gain).astype(jnp.bfloat16)
    key_rope = rotary(compressed[:, LATENT:], query_pos).astype(jnp.bfloat16)
    n_tok = lax.axis_size("tok")
    reach = LONGEST_SEGMENT // tok_dev
    kv_own = jnp.concatenate([latent, key_rope], axis=-1)
    kv_parts = [kv_own]
    earlier = {}
    for steps in range(min(reach, n_tok - 1), 0, -1):
        earlier[steps] = passed_along(kv_own, "tok", steps)
    for steps in range(1, min(reach, n_tok - 1) + 1):
        kv_parts.insert(0, earlier[steps])
    kv_rows = jnp.concatenate(kv_parts, axis=0)
    key_count = kv_rows.shape[0]
    key_start = query_start + tok_dev - key_count
    expanded = (
        jnp.dot(kv_rows[:, :LATENT], w_kv_up, preferred_element_type=jnp.float32)
        .astype(jnp.bfloat16)
        .reshape(key_count, local_heads, NOPE + VDIM)
    )
    rope_keys = kv_rows[:, LATENT:]
    scores = jnp.einsum(
        "hdq,khd->hqk", queries_t[:, :NOPE], expanded[..., :NOPE],
        preferred_element_type=jnp.float32,
    )
    scores = scores + jnp.einsum(
        "hdq,kd->hqk", queries_t[:, NOPE:], rope_keys, preferred_element_type=jnp.float32
    )
    scores = scores * score_scale
    key_index = key_start + jnp.arange(key_count, dtype=jnp.int32)
    padded_seg = jnp.concatenate([jnp.full((key_count,), -1, jnp.int32), segment_row])
    key_seg = lax.dynamic_slice_in_dim(padded_seg, key_start + key_count, key_count)
    allowed = (
        (key_seg[None, :] == query_seg[:, None])
        & (key_index[None, :] <= query_index[:, None])
        & (key_index[None, :] >= 0)
    )
    allowed = allowed[None, :, :]
    masked = jnp.where(allowed, scores, -1e30)
    row_max = jnp.max(masked, axis=-1, keepdims=True)
    weights = jnp.where(allowed, jnp.exp(scores - row_max), 0.0)
    totals = jnp.sum(weights, axis=-1, keepdims=True)
    weighted = jnp.einsum(
        "hqk,khd->hqd", weights.astype(jnp.bfloat16), expanded[..., NOPE:],
        preferred_element_type=jnp.float32,
    )
    attended = (
        (weighted / totals).astype(jnp.bfloat16).transpose(1, 0, 2).reshape(tok_dev, local_heads * VDIM)
    )
    head_parts = jnp.dot(attended, w_out, preferred_element_type=jnp.float32).astype(jnp.bfloat16)
    mixed_heads = summed_over(head_parts, "mdl")
    own_input = lax.dynamic_slice_in_dim(rows_in, mdl_rank * row_dev, row_dev)
    own_residual = (own_input.astype(jnp.float32) + mixed_heads).astype(jnp.bfloat16)
    normed_ffn = rms_scale(own_residual, ffn_gain).astype(jnp.bfloat16)
    normed_ffn_all = gathered_over(normed_ffn, "mdl")

    gate_proj = jnp.dot(normed_ffn_all, w_shared_gate, preferred_element_type=jnp.float32)
    up_proj = jnp.dot(normed_ffn_all, w_shared_up, preferred_element_type=jnp.float32)
    shared_act = (jax.nn.silu(gate_proj) * up_proj).astype(jnp.bfloat16)
    shared_out = summed_over(
        jnp.dot(shared_act, w_shared_down, preferred_element_type=jnp.float32).astype(jnp.bfloat16),
        "mdl",
        arrival_order=True,
    )

    onehot = (expert_ids[:, None] == expert_labels[None, :]).astype(jnp.int32)
    earlier = jnp.cumsum(onehot, axis=0) - onehot
    slot_index = jnp.sum(earlier * onehot, axis=1)
    target = expert_ids * capacity + slot_index
    placing = (
        (slot_ids[:, None] == target[None, :])
        .astype(jnp.int32)
        .reshape(slot_total, row_dev, top_count)
    )
    placing = (
        jnp.sum(placing, axis=2)
        .astype(jnp.bfloat16)
        .reshape(n_wide, expert_dev, capacity, row_dev)
    )
    outgoing = jnp.einsum(
        "sjkr,rd->sjkd", placing, normed_ffn, preferred_element_type=jnp.float32
    ).astype(jnp.bfloat16)
    buffer = lax.all_to_all(outgoing, ("tok", "mdl"), split_axis=0, concat_axis=0, tiled=True)
    e_gate = jnp.einsum("sjkd,jdf->sjkf", buffer, w_expert_gate, preferred_element_type=jnp.float32)
    e_up = jnp.einsum("sjkd,jdf->sjkf", buffer, w_expert_up, preferred_element_type=jnp.float32)
    expert_act = (jax.nn.silu(e_gate) * e_up).astype(jnp.bfloat16)
    produced = jnp.einsum(
        "sjkf,jfd->sjkd", expert_act, w_expert_down, preferred_element_type=jnp.float32
    ).astype(jnp.bfloat16)
    returned = lax.all_to_all(produced, ("tok", "mdl"), split_axis=0, concat_axis=0, tiled=True)
    matched = target.reshape(row_dev, top_count)[:, :, None] == slot_ids[None, None, :]
    combining = jnp.sum(jnp.where(matched, weight_rows[:, :, None], 0.0), axis=1).reshape(
        row_dev, n_wide, expert_dev, capacity
    )
    routed = jnp.einsum(
        "rsjk,sjkd->rd",
        combining,
        returned.astype(jnp.float32),
        precision=lax.Precision.HIGH,
    )
    finished = (own_residual.astype(jnp.float32) + shared_out + routed).astype(jnp.bfloat16)
    return finished[None]


def solution(mesh):
    in_specs = (
        P(None, "tok", None),
        P(),
        P(None, ("tok", "mdl"), None),
        P(None, ("tok", "mdl"), None),
        P(),
        P(None, "mdl"),
        P(),
        P(),
        P(None, "mdl"),
        P("mdl", None),
        P(),
        P(None, "mdl"),
        P(None, "mdl"),
        P("mdl", None),
        P(("tok", "mdl"), None, None),
        P(("tok", "mdl"), None, None),
        P(("tok", "mdl"), None, None),
    )
    out_specs = P("section", ("tok", "mdl"), None)
    return jax.shard_map(shards, mesh=mesh, in_specs=in_specs, out_specs=out_specs, check_vma=False)
```
